256 devices in a mesh: wide: 32 (over y, z), deep: 8 (over x, core).
Axes of the slice: x: 4, y: 4, z: 8, core: 2. Of those that a mesh axis runs over, the one named last changes fastest.
Arguments:
- rhs_local: float32 [512, 128, 256], P('wide', 'deep'), may hold values from -6 to 6
- metric: float32 [3, 512, 128, 256], P(None, 'wide', 'deep'), may hold values from 0.005 to 0.05
- helm: float32 [512, 128, 256], P('wide', 'deep'), may hold values from 0.5 to 4
- columns: int32 [32, 16, 8, 8], P('wide', 'deep'), may hold values from 0 to 47
- live_blocks: int32 [32, 16, 8], P('wide', 'deep'), may hold values from 1 to 8
- block_values: float32 [32, 16, 8, 512], P('wide', 'deep'), may hold values from -0.0234375 to 0.0234375
Outputs:
- smoothed: float32 [512, 128, 256], P('wide', 'deep')
- coarse_product: float32 [32, 16, 64], P('wide', 'deep')
The draws below stay inside these ranges and needn't reach their ends.
All inputs are finite; a program needn't handle non-finite values.
Results may differ from the reference program's by a relative error of at most 0.00013.
Values sent between devices are 32-bit elements; how exact they have to be, the bound alone decides.
No kernel may reach another device: no remote copies, remote signals or barrier semaphores. Data moves between devices by JAX's collectives and lax.ppermute only.
A program may use at most 64 MiB of HBM per device.

```python
import math
import jax
import jax.numpy as jnp
import numpy as np
from jax import lax

NP = 8
EY = 2
ZL = 1
DEGREE = 2
K = 8
BS = 8
EZ = 32
NXV = 64
NYV = 16
NXB = 8
NBL = 16
NX = 512
NY = 128
NZ = 256
N_WIDE = 32
N_DEEP = 8


def draw_live_blocks(key, part):
    counts = jax.random.randint(key, (EZ, NYV, NXB), 1, K + 1)
    return counts.at[0, 0, 0].set(K).astype(jnp.int32)


def plant(entries, own_key, least, top_value):
    dims = entries.shape
    place = [jax.random.randint(jax.random.fold_in(own_key, axis), (), 0, dims[axis]) for axis in range(len(dims))]
    entries = entries.at[tuple(place)].set(least)
    longest = dims.index(max(dims))
    place[longest] = (place[longest] + 1) % dims[longest]
    return entries.at[tuple(place)].set(top_value)


def steps_of(key, shape, cuts, least, largest):
    loudness = 1.0
    for dim, shards_of in cuts:
        steps = jax.random.uniform(jax.random.fold_in(jax.random.fold_in(key, 6), dim), (shards_of,), jnp.float32, least / len(cuts), largest / len(cuts))
        loudness = loudness * jnp.repeat(jnp.exp(steps), shape[dim] // shards_of).reshape((-1,) + (1,) * (len(shape) - 1 - dim))
    return loudness


def scatter_about(stream_key, shape, deviation, limit, shards=(), kind=jnp.bfloat16):
    drawn = jax.random.normal(stream_key, shape, jnp.float32) * deviation
    if len(shards) > 0:
        drawn = steps_of(stream_key, shape, shards, -0.22, 0.18) * drawn
    return jnp.clip(drawn, min=-limit, max=limit).astype(kind)


def setup_inputs(seed: int = 0) -> dict:
    arg_keys = jax.random.split(jax.random.key(seed), 7)
    return {
        "rhs_local": scatter_about(arg_keys[0], (NX, NY, NZ), 1.0, 6.0, ((0, 32), (1, 8)), jnp.float32),
        "metric": jnp.clip(jnp.exp(math.log(0.05) - 2.3025851 * jax.random.uniform(arg_keys[1], (3, NX, NY, NZ), jnp.float32) ** steps_of(arg_keys[1], (3, NX, NY, NZ), ((1, 32), (2, 8)), -0.2, 0.2)), 0.005, 0.05),
        "helm": jnp.clip(jnp.exp(math.log(4.0) - 2.0794415 * jax.random.uniform(arg_keys[2], (NX, NY, NZ), jnp.float32) ** steps_of(arg_keys[2], (NX, NY, NZ), ((0, 32), (1, 8)), -0.2, 0.2)), 0.5, 4.0),
        "columns": plant(jax.random.randint(arg_keys[3], (EZ, NYV, NXB, K), 0, 3 * NBL), jax.random.fold_in(arg_keys[3], 1), 0, (3 * NBL) - 1).astype(jnp.int32),
        "live_blocks": draw_live_blocks(jax.random.fold_in(arg_keys[6], 71), 0),
        "block_values": scatter_about(arg_keys[5], (EZ, NYV, NXB, K * BS * BS), (2 * K * BS * NP**3) ** -0.5, 0.0234375, ((0, 32), (1, 8)), jnp.float32),
    }


upper_bound = 6.0
lower_bound = 0.6
highest = lax.Precision.HIGHEST
forward_forms = ("mi,aibjck->ambjck", "mj,aibjck->aibmck", "mk,aibjck->aibjcm")
backward_forms = ("mi,ambjck->aibjck", "mj,aibmck->aibjck", "mk,aibjcm->aibjck")


def gll_tables(count):
    order = count - 1
    nodes = np.cos(np.pi * np.arange(count) / order)
    legendre = np.zeros((count, count))
    for sweep in range(101):
        legendre[:, 0] = 1.0
        legendre[:, 1] = nodes
        for degree in range(2, count):
            legendre[:, degree] = ((2 * degree - 1) * nodes * legendre[:, degree - 1] - (degree - 1) * legendre[:, degree - 2]) / degree
        if sweep < 100:
            nodes = nodes - (nodes * legendre[:, order] - legendre[:, order - 1]) / (count * legendre[:, order])
    nodes = nodes[::-1].copy()
    values = legendre[::-1, order].copy()
    identity_table = np.eye(count)
    spacing = nodes[:, None] - nodes[None, :] + identity_table
    derivative = values[:, None] / values[None, :] / spacing
    derivative = derivative * (1.0 - identity_table)
    derivative[0, 0] = -order * (order + 1) / 4.0
    derivative[-1, -1] = order * (order + 1) / 4.0
    linear = np.stack([(1.0 - nodes) / 2.0, (1.0 + nodes) / 2.0], axis=1)
    return jnp.asarray(derivative, jnp.float32), jnp.asarray(linear, jnp.float32)


def as_elements(field, count):
    shape = field.shape
    return field.reshape(shape[0] // count, count, shape[1] // count, count, shape[2] // count, count)


def pair_sum(grid, axis, wrap):
    node_axis = 2 * axis + 1
    elem_axis = 2 * axis
    count = grid.shape[node_axis]
    first = lax.slice_in_dim(grid, 0, 1, axis=node_axis)
    inner = lax.slice_in_dim(grid, 1, count - 1, axis=node_axis)
    last = lax.slice_in_dim(grid, count - 1, count, axis=node_axis)
    if wrap:
        shared = last + jnp.roll(first, -1, axis=elem_axis)
        new_last = shared
        new_first = jnp.roll(shared, 1, axis=elem_axis)
    else:
        length = last.shape[elem_axis]
        shared = lax.slice_in_dim(last, 0, length - 1, axis=elem_axis) + lax.slice_in_dim(first, 1, length, axis=elem_axis)
        new_last = jnp.concatenate([shared, lax.slice_in_dim(last, length - 1, length, axis=elem_axis)], axis=elem_axis)
        new_first = jnp.concatenate([lax.slice_in_dim(first, 0, 1, axis=elem_axis), shared], axis=elem_axis)
    return jnp.concatenate([new_first, inner, new_last], axis=node_axis)


def assemble(field, count):
    grid = as_elements(field, count)
    for axis in range(3):
        grid = pair_sum(grid, axis, True)
    return grid.reshape(field.shape)


def apply_operator(field, metric, helm, derivative):
    count = derivative.shape[0]
    grid = as_elements(field, count)
    total = helm * field
    for axis in range(3):
        slope = jnp.einsum(forward_forms[axis], derivative, grid, precision=highest)
        flux = as_elements(metric[axis], count) * slope
        total = total + jnp.einsum(backward_forms[axis], derivative, flux, precision=highest).reshape(field.shape)
    return total


def operator_diagonal(metric, helm, derivative):
    count = derivative.shape[0]
    squares = derivative * derivative
    total = helm
    for axis in range(3):
        total = total + jnp.einsum(backward_forms[axis], squares, as_elements(metric[axis], count), precision=highest).reshape(helm.shape)
    return total


def chebyshev(solution, rhs_local, metric, helm, derivative, inverse, from_zero):
    centre = (upper_bound + lower_bound) / 2.0
    half_width = (upper_bound - lower_bound) / 2.0
    aspect = centre / half_width
    weight_prev = 1.0 / aspect
    if from_zero:
        residual = assemble(rhs_local, NP)
    else:
        residual = assemble(rhs_local - apply_operator(solution, metric, helm, derivative), NP)
    update = inverse * residual / centre
    solution = solution + update
    for turn in range(DEGREE - 1):
        residual = assemble(rhs_local - apply_operator(solution, metric, helm, derivative), NP)
        weight_next = 1.0 / (2.0 * aspect - weight_prev)
        update = weight_next * weight_prev * update + (2.0 * weight_next / half_width) * inverse * residual
        solution = solution + update
        weight_prev = weight_next
    return solution


def restrict(field, linear, count):
    grid = as_elements(field, count)
    small = jnp.einsum("ia,jb,kc,xiyjzk->xaybzc", linear, linear, linear, grid, precision=highest)
    shape = field.shape
    return small.reshape(shape[0] // count * 2, shape[1] // count * 2, shape[2] // count * 2)


def prolong_values(vertices, linear):
    shape = vertices.shape
    holder = jnp.zeros((shape[0], 2, shape[1], 2, shape[2], 2), jnp.float32)
    holder = holder.at[:, 0, :, 0, :, 0].set(vertices)
    summed = assemble(holder.reshape(shape[0] * 2, shape[1] * 2, shape[2] * 2), 2)
    grid = jnp.einsum("ia,jb,kc,xaybzc->xiyjzk", linear, linear, linear, as_elements(summed, 2), precision=highest)
    count = linear.shape[0]
    return grid.reshape(shape[0] * count, shape[1] * count, shape[2] * count)


def coarse_multiply(coarse_res, columns, live_blocks, block_values):
    owners = N_WIDE
    groups = N_DEEP
    per_owner = ZL * EY * NXB
    vectors = coarse_res.reshape(owners, ZL, groups, EY, NXB, BS).transpose(0, 2, 1, 3, 4, 5).reshape(owners, groups, per_owner, BS)
    frame = jnp.concatenate([jnp.roll(vectors, 1, axis=0), vectors, jnp.roll(vectors, -1, axis=0)], axis=2)
    frame_rows = frame.reshape(owners * groups * 3 * per_owner, BS)
    index = columns.reshape(owners, ZL, groups, EY, NXB, K).transpose(0, 2, 1, 3, 4, 5).reshape(owners, groups, per_owner * K)
    offsets = (jnp.arange(owners * groups, dtype=jnp.int32) * (3 * per_owner)).reshape(owners, groups, 1)
    picked = jnp.take(frame_rows, (index + offsets).reshape(-1), axis=0).reshape(owners, groups, per_owner, K, BS)
    counts = live_blocks.reshape(owners, ZL, groups, EY, NXB).transpose(0, 2, 1, 3, 4).reshape(owners, groups, per_owner)
    live = (jnp.arange(K, dtype=jnp.int32)[None, None, None, :] < counts[:, :, :, None]).astype(jnp.float32)
    values = block_values.reshape(owners, ZL, groups, EY, NXB, K, BS, BS).transpose(0, 2, 1, 3, 4, 5, 6, 7).reshape(owners, groups, per_owner, K, BS, BS)
    product = jnp.einsum("wdlkij,wdlkj,wdlk->wdli", values, picked, live, precision=highest)
    return product.reshape(owners, groups, ZL, EY, NXB, BS).transpose(0, 2, 1, 3, 4, 5).reshape(EZ, NYV, NXV)


def reference(rhs_local, metric, helm, columns, live_blocks, block_values):
    derivative, linear = gll_tables(NP)
    inverse = 1.0 / assemble(operator_diagonal(metric, helm, derivative), NP)
    first = chebyshev(jnp.zeros_like(rhs_local), rhs_local, metric, helm, derivative, inverse, True)
    local_res = rhs_local - apply_operator(first, metric, helm, derivative)
    assembled = assemble(restrict(local_res, linear, NP), 2)
    vertices = as_elements(assembled, 2)[:, 0, :, 0, :, 0]
    coarse_res = jnp.transpose(vertices, (2, 1, 0))
    coarse_product = coarse_multiply(coarse_res, columns, live_blocks, block_values)
    second = first + prolong_values(jnp.transpose(coarse_product, (2, 1, 0)), linear)
    smoothed = chebyshev(second, rhs_local, metric, helm, derivative, inverse, False)
    return smoothed, coarse_product
```

```python
import jax
import jax.numpy as jnp
import numpy as np
from jax import lax
from jax.sharding import PartitionSpec as P

NP = 8
K = 8
BS = 8


upper_bound = 6.0
lower_bound = 0.6
highest = lax.Precision.HIGHEST


def gll_tables(count):
    order = count - 1
    nodes = np.cos(np.pi * np.arange(count) / order)
    legendre = np.zeros((count, count))
    for sweep in range(101):
        legendre[:, 0] = 1.0
        legendre[:, 1] = nodes
        for degree in range(2, count):
            legendre[:, degree] = (
                (2 * degree - 1) * nodes * legendre[:, degree - 1]
                - (degree - 1) * legendre[:, degree - 2]
            ) / degree
        if sweep < 100:
            nodes = nodes - (nodes * legendre[:, order] - legendre[:, order - 1]) / (
                count * legendre[:, order]
            )
    nodes = nodes[::-1].copy()
    values = legendre[::-1, order].copy()
    identity_table = np.eye(count)
    spacing = nodes[:, None] - nodes[None, :] + identity_table
    derivative = values[:, None] / values[None, :] / spacing
    derivative = derivative * (1.0 - identity_table)
    derivative[0, 0] = -order * (order + 1) / 4.0
    derivative[-1, -1] = order * (order + 1) / 4.0
    linear = np.stack([(1.0 - nodes) / 2.0, (1.0 + nodes) / 2.0], axis=1)
    return (np.asarray(derivative, np.float32), np.asarray(linear, np.float32))


def block_extent():
    return 128


def repeat_table(small, copies):
    return jnp.asarray(np.kron(np.eye(copies, dtype=np.float32), small))


def contract(field, table, axis):
    if axis == 0:
        return jnp.einsum("mi,iyz->myz", table, field, precision=highest)
    if axis == 1:
        return jnp.einsum("mj,xjz->xmz", table, field, precision=highest)
    shape = field.shape
    blocked = table.shape[1]
    grid = field.reshape(shape[0], shape[1], shape[2] // blocked, blocked)
    result = jnp.einsum("mk,xynk->xynm", table, grid, precision=highest)
    return result.reshape(shape[0], shape[1], -1)


def shift(value, dw, dd):
    nw = lax.axis_size("wide")
    nd = lax.axis_size("deep")
    if dd == 0:
        pairs = [((w + dw) % nw, w) for w in range(nw)]
        return lax.ppermute(value, "wide", pairs)
    if dw == 0:
        pairs = [((d + dd) % nd, d) for d in range(nd)]
        return lax.ppermute(value, "deep", pairs)
    pairs = []
    for w in range(nw):
        for d in range(nd):
            src = ((w + dw) % nw) * nd + (d + dd) % nd
            pairs.append((src, w * nd + d))
    return lax.ppermute(value, ("wide", "deep"), pairs)


def node_mask(length, count, node, axis, ndim):
    index = lax.broadcasted_iota(jnp.int32, (length,), 0) % count == node
    shape = [1] * ndim
    shape[axis] = length
    return index.reshape(shape)


def assemble(field, count):
    nd = field.ndim
    lx = shift(field[..., -1, :, :], -1, 0)
    rx = shift(field[..., 0, :, :], 1, 0)
    ly = shift(field[..., :, -1, :], 0, -1)
    ry = shift(field[..., :, 0, :], 0, 1)
    ll = shift(field[..., -1, -1, :], -1, -1)
    lr = shift(field[..., -1, 0, :], -1, 1)
    rl = shift(field[..., 0, -1, :], 1, -1)
    rr = shift(field[..., 0, 0, :], 1, 1)
    top = jnp.concatenate([ll[..., None, :], lx, lr[..., None, :]], axis=-2)
    mid = jnp.concatenate([ly[..., :, None, :], field, ry[..., :, None, :]], axis=-2)
    bot = jnp.concatenate([rl[..., None, :], rx, rr[..., None, :]], axis=-2)
    ext = jnp.concatenate([top[..., None, :, :], mid, bot[..., None, :, :]], axis=-3)
    X, Y, Z = field.shape[-3:]
    hi = node_mask(X, count, count - 1, nd - 3, nd)
    lo = node_mask(X, count, 0, nd - 3, nd)
    ext = (
        ext[..., 1 : X + 1, :, :]
        + jnp.where(hi, ext[..., 2 : X + 2, :, :], 0.0)
        + jnp.where(lo, ext[..., 0:X, :, :], 0.0)
    )
    hi = node_mask(Y, count, count - 1, nd - 2, nd)
    lo = node_mask(Y, count, 0, nd - 2, nd)
    ext = (
        ext[..., :, 1 : Y + 1, :]
        + jnp.where(hi, ext[..., :, 2 : Y + 2, :], 0.0)
        + jnp.where(lo, ext[..., :, 0:Y, :], 0.0)
    )
    hi = node_mask(Z, count, count - 1, nd - 1, nd)
    lo = node_mask(Z, count, 0, nd - 1, nd)
    return (
        ext
        + jnp.where(hi, jnp.roll(ext, -1, axis=-1), 0.0)
        + jnp.where(lo, jnp.roll(ext, 1, axis=-1), 0.0)
    )


def apply_operator(field, metric, helm, tables):
    total = helm * field
    for axis in range(3):
        slope = contract(field, tables[axis], axis)
        total = total + contract(metric[axis] * slope, tables[axis].T, axis)
    return total


def chebyshev(solution, rhs_local, metric, helm, tables, inverse, first_residual):
    centre = (upper_bound + lower_bound) / 2.0
    half_width = (upper_bound - lower_bound) / 2.0
    aspect = centre / half_width
    weight_prev = 1.0 / aspect
    if first_residual is not None:
        residual = first_residual
    else:
        residual = assemble(rhs_local - apply_operator(solution, metric, helm, tables), NP)
    update = inverse * residual / centre
    solution = solution + update
    residual = assemble(rhs_local - apply_operator(solution, metric, helm, tables), NP)
    weight_next = 1.0 / (2.0 * aspect - weight_prev)
    update = (
        weight_next * weight_prev * update + 2.0 * weight_next / half_width * inverse * residual
    )
    solution = solution + update
    return solution


def local(rhs_local, metric, helm, columns, live_blocks, block_values):
    derivative, linear = gll_tables(NP)
    shape = rhs_local.shape
    nw = lax.axis_size("wide")
    copies = (shape[0] // NP, shape[1] // NP, block_extent() // NP)
    tables = tuple((repeat_table(derivative, copies[axis]) for axis in range(3)))
    square_tables = tuple(
        (repeat_table(derivative * derivative, copies[axis]) for axis in range(3))
    )
    down_tables = tuple((repeat_table(linear.T, copies[axis]) for axis in range(3)))
    up_tables = tuple((repeat_table(linear, copies[axis]) for axis in range(3)))

    next_columns = shift(columns[0, 0].astype(jnp.float32), 0, 1).astype(jnp.int32)
    next_live = shift(live_blocks[0, 0].astype(jnp.float32), 0, 1).astype(jnp.int32)
    next_values = shift(block_values[0, 0], 0, 1)

    diagonal = helm
    for axis in range(3):
        diagonal = diagonal + contract(metric[axis], square_tables[axis].T, axis)
    both = assemble(jnp.stack([diagonal, rhs_local]), NP)
    inverse = 1.0 / both[0]
    first = chebyshev(
        jnp.zeros_like(rhs_local), rhs_local, metric, helm, tables, inverse, both[1]
    )
    local_res = rhs_local - apply_operator(first, metric, helm, tables)
    corners = local_res
    for axis in range(3):
        corners = contract(corners, down_tables[axis], axis)

    cx, cy, cz = corners.shape
    rows = []
    for dw in (-1, 0):
        cols_ = []
        for dd in (-1, 0, 1):
            cols_.append(corners if (dw, dd) == (0, 0) else shift(corners, dw, dd))
        rows.append(jnp.concatenate(cols_, axis=1))
    ext = jnp.concatenate(rows, axis=0)
    qz = ext[:, :, 0::2] + jnp.roll(ext, 1, axis=2)[:, :, 0::2]
    qx = qz[cx : cx + 3 : 2] + qz[cx - 1 : cx + 2 : 2]
    vertices = qx[:, cy : cy + 7 : 2] + qx[:, cy - 1 : cy + 6 : 2]

    sent = jnp.stack(
        [jnp.roll(vertices, 1, axis=2), vertices, jnp.roll(vertices, -1, axis=2)], axis=-1
    )
    sent = jnp.transpose(sent, (2, 0, 1, 3))
    got = lax.all_to_all(sent, "wide", 0, 0, tiled=True)
    frame = jnp.transpose(got, (3, 2, 0, 1)).reshape(3, 4, -1)
    span = frame.shape[2]
    nxb = span // BS
    frame_rows = frame.reshape(-1, BS)

    cols = jnp.concatenate([columns[0], next_columns[None]], axis=0)
    lives = jnp.concatenate([live_blocks[0], next_live[None]], axis=0)
    vals = jnp.concatenate([block_values[0], next_values[None]], axis=0)
    y_off = jnp.array([0, 0, 2], jnp.int32)[:, None, None]
    layer = cols // (2 * nxb)
    block = cols % (2 * nxb)
    index = (layer * 4 + y_off + block // nxb) * nxb + block % nxb
    picked = jnp.take(frame_rows, index.reshape(-1), axis=0).reshape(index.shape + (BS,))
    live = (jnp.arange(K, dtype=jnp.int32)[None, None, :] < lives[:, :, None]).astype(
        jnp.float32
    )
    values = vals.reshape(vals.shape[:2] + (K, BS, BS))
    product = jnp.einsum("yxkij,yxkj,yxk->yxi", values, picked, live, precision=highest)
    product = product.reshape(3, span)
    coarse_product = product[:2].reshape(1, 2, span)

    pick = (2 * np.arange(nw)[:, None] + np.arange(3)[None, :]) % span
    back = jnp.transpose(product[:, pick], (1, 0, 2))
    got = lax.all_to_all(back, "wide", 0, 0, tiled=True)
    hx = jnp.stack([got[:, :, 0:2], got[:, :, 1:3]], axis=-1).reshape(nw, 3, 4)
    hy = jnp.stack([hx[:, 0:2], hx[:, 1:3]], axis=2).reshape(nw, 4, 4)
    hz = jnp.stack([hy, jnp.roll(hy, -1, axis=0)], axis=1).reshape(2 * nw, 4, 4)
    correction = jnp.transpose(hz, (2, 1, 0))
    for axis in range(3):
        correction = contract(correction, up_tables[axis], axis)
    second = first + correction
    smoothed = chebyshev(second, rhs_local, metric, helm, tables, inverse, None)
    return (smoothed, coarse_product)


def solution(mesh):
    placed = (
        P("wide", "deep", None),
        P(None, "wide", "deep", None),
        P("wide", "deep", None),
        P("wide", "deep", None, None),
        P("wide", "deep", None),
        P("wide", "deep", None, None),
    )
    return jax.shard_map(
        local,
        mesh=mesh,
        in_specs=placed,
        out_specs=(P("wide", "deep", None), P("wide", "deep", None)),
        check_vma=False,
    )
```

```python
import jax
import jax.numpy as jnp
import numpy as np
from jax import lax
from jax.sharding import PartitionSpec as P

NP = 8
K = 8
BS = 8


upper_bound = 6.0
lower_bound = 0.6
highest = lax.Precision.HIGHEST


def gll_tables(count):
    order = count - 1
    nodes = np.cos(np.pi * np.arange(count) / order)
    legendre = np.zeros((count, count))
    for sweep in range(101):
        legendre[:, 0] = 1.0
        legendre[:, 1] = nodes
        for degree in range(2, count):
            legendre[:, degree] = (
                (2 * degree - 1) * nodes * legendre[:, degree - 1]
                - (degree - 1) * legendre[:, degree - 2]
            ) / degree
        if sweep < 100:
            nodes = nodes - (nodes * legendre[:, order] - legendre[:, order - 1]) / (
                count * legendre[:, order]
            )
    nodes = nodes[::-1].copy()
    values = legendre[::-1, order].copy()
    identity_table = np.eye(count)
    spacing = nodes[:, None] - nodes[None, :] + identity_table
    derivative = values[:, None] / values[None, :] / spacing
    derivative = derivative * (1.0 - identity_table)
    derivative[0, 0] = -order * (order + 1) / 4.0
    derivative[-1, -1] = order * (order + 1) / 4.0
    linear = np.stack([(1.0 - nodes) / 2.0, (1.0 + nodes) / 2.0], axis=1)
    return (np.asarray(derivative, np.float32), np.asarray(linear, np.float32))


def block_extent():
    return 128


def repeat_table(small, copies):
    return jnp.asarray(np.kron(np.eye(copies, dtype=np.float32), small))


def contract(field, table, axis):
    if axis == 0:
        return jnp.einsum("mi,iyz->myz", table, field, precision=highest)
    if axis == 1:
        return jnp.einsum("mj,xjz->xmz", table, field, precision=highest)
    shape = field.shape
    blocked = table.shape[1]
    grid = field.reshape(shape[0], shape[1], shape[2] // blocked, blocked)
    result = jnp.einsum("mk,xynk->xynm", table, grid, precision=highest)
    return result.reshape(shape[0], shape[1], -1)


def shift(value, dw, dd):
    nw = lax.axis_size("wide")
    nd = lax.axis_size("deep")
    if dd == 0:
        pairs = [((w + dw) % nw, w) for w in range(nw)]
        return lax.ppermute(value, "wide", pairs)
    if dw == 0:
        pairs = [((d + dd) % nd, d) for d in range(nd)]
        return lax.ppermute(value, "deep", pairs)
    pairs = []
    for w in range(nw):
        for d in range(nd):
            src = ((w + dw) % nw) * nd + (d + dd) % nd
            pairs.append((src, w * nd + d))
    return lax.ppermute(value, ("wide", "deep"), pairs)


def node_mask(length, count, node, axis, ndim):
    index = lax.broadcasted_iota(jnp.int32, (length,), 0) % count == node
    shape = [1] * ndim
    shape[axis] = length
    return index.reshape(shape)


def assemble(field, count, carry=None):
    nd = field.ndim
    X, Y, Z = field.shape[-3:]
    lx = shift(field[..., -1, :, :], -1, 0)
    rx = shift(field[..., 0, :, :], 1, 0)
    ext = jnp.concatenate([lx[..., None, :, :], field, rx[..., None, :, :]], axis=-3)
    hi = node_mask(X, count, count - 1, nd - 3, nd)
    lo = node_mask(X, count, 0, nd - 3, nd)
    field = (
        ext[..., 1 : X + 1, :, :]
        + jnp.where(hi, ext[..., 2 : X + 2, :, :], 0.0)
        + jnp.where(lo, ext[..., 0:X, :, :], 0.0)
    )
    ly = shift(field[..., :, -1, :], 0, -1)
    face = field[..., :, 0, :]
    carried = None
    if carry is None:
        ry = shift(face, 0, 1)
    else:
        packed = shift(jnp.concatenate([face.reshape(-1), carry]), 0, 1)
        ry = packed[: face.size].reshape(face.shape)
        carried = packed[face.size :]
    ext = jnp.concatenate([ly[..., :, None, :], field, ry[..., :, None, :]], axis=-2)
    hi = node_mask(Y, count, count - 1, nd - 2, nd)
    lo = node_mask(Y, count, 0, nd - 2, nd)
    field = (
        ext[..., :, 1 : Y + 1, :]
        + jnp.where(hi, ext[..., :, 2 : Y + 2, :], 0.0)
        + jnp.where(lo, ext[..., :, 0:Y, :], 0.0)
    )
    hi = node_mask(Z, count, count - 1, nd - 1, nd)
    lo = node_mask(Z, count, 0, nd - 1, nd)
    field = (
        field
        + jnp.where(hi, jnp.roll(field, -1, axis=-1), 0.0)
        + jnp.where(lo, jnp.roll(field, 1, axis=-1), 0.0)
    )
    if carry is None:
        return field
    return field, carried


def apply_operator(field, metric, helm, tables):
    total = helm * field
    for axis in range(3):
        slope = contract(field, tables[axis], axis)
        total = total + contract(metric[axis] * slope, tables[axis].T, axis)
    return total


def chebyshev(solution, rhs_local, metric, helm, tables, inverse, first_residual):
    centre = (upper_bound + lower_bound) / 2.0
    half_width = (upper_bound - lower_bound) / 2.0
    aspect = centre / half_width
    weight_prev = 1.0 / aspect
    if first_residual is not None:
        residual = first_residual
    else:
        residual = assemble(rhs_local - apply_operator(solution, metric, helm, tables), NP)
    update = inverse * residual / centre
    solution = solution + update
    residual = assemble(rhs_local - apply_operator(solution, metric, helm, tables), NP)
    weight_next = 1.0 / (2.0 * aspect - weight_prev)
    update = (
        weight_next * weight_prev * update + 2.0 * weight_next / half_width * inverse * residual
    )
    solution = solution + update
    return solution


def local(rhs_local, metric, helm, columns, live_blocks, block_values):
    derivative, linear = gll_tables(NP)
    shape = rhs_local.shape
    nw = lax.axis_size("wide")
    copies = (shape[0] // NP, shape[1] // NP, block_extent() // NP)
    tables = tuple((repeat_table(derivative, copies[axis]) for axis in range(3)))
    square_tables = tuple(
        (repeat_table(derivative * derivative, copies[axis]) for axis in range(3))
    )
    down_tables = tuple((repeat_table(linear.T, copies[axis]) for axis in range(3)))
    up_tables = tuple((repeat_table(linear, copies[axis]) for axis in range(3)))

    diagonal = helm
    for axis in range(3):
        diagonal = diagonal + contract(metric[axis], square_tables[axis].T, axis)
    mats = jnp.concatenate(
        [
            block_values[0, 0].reshape(-1),
            columns[0, 0].astype(jnp.float32).reshape(-1),
            live_blocks[0, 0].astype(jnp.float32),
        ]
    )
    both, mats = assemble(jnp.stack([diagonal, rhs_local]), NP, mats)
    nvals = block_values.shape[2] * block_values.shape[3]
    ncols = columns.shape[2] * columns.shape[3]
    next_values = mats[:nvals].reshape(block_values.shape[2:])
    next_columns = mats[nvals : nvals + ncols].astype(jnp.int32).reshape(columns.shape[2:])
    next_live = mats[nvals + ncols :].astype(jnp.int32)
    inverse = 1.0 / both[0]
    first = chebyshev(
        jnp.zeros_like(rhs_local), rhs_local, metric, helm, tables, inverse, both[1]
    )
    local_res = rhs_local - apply_operator(first, metric, helm, tables)
    corners = local_res
    for axis in range(3):
        corners = contract(corners, down_tables[axis], axis)

    cx, cy, cz = corners.shape
    ext = jnp.concatenate([shift(corners, 0, -1), corners, shift(corners, 0, 1)], axis=1)
    qz = ext[:, :, 0::2] + jnp.roll(ext, 1, axis=2)[:, :, 0::2]
    qy = qz[:, cy : cy + 7 : 2] + qz[:, cy - 1 : cy + 6 : 2]
    zero = jnp.zeros_like(qy[:1])
    qx = jnp.concatenate([zero, qy, zero], axis=0)
    partial = qx[1 : cx + 2 : 2] + qx[0 : cx + 1 : 2]

    sent = jnp.stack(
        [jnp.roll(partial, 1, axis=2), partial, jnp.roll(partial, -1, axis=2)], axis=-1
    )
    sent = jnp.transpose(sent, (2, 0, 1, 3))
    got = lax.all_to_all(sent, "wide", 0, 0, tiled=True)
    even = got[:, 0] + jnp.roll(got[:, 2], 1, axis=0)
    got = jnp.stack([even, got[:, 1]], axis=1)
    frame = jnp.transpose(got, (3, 2, 0, 1)).reshape(3, 4, -1)
    span = frame.shape[2]
    nxb = span // BS
    frame_rows = frame.reshape(-1, BS)

    cols = jnp.concatenate([columns[0], next_columns[None]], axis=0)
    lives = jnp.concatenate([live_blocks[0], next_live[None]], axis=0)
    vals = jnp.concatenate([block_values[0], next_values[None]], axis=0)
    y_off = jnp.array([0, 0, 2], jnp.int32)[:, None, None]
    layer = cols // (2 * nxb)
    block = cols % (2 * nxb)
    index = (layer * 4 + y_off + block // nxb) * nxb + block % nxb
    picked = jnp.take(frame_rows, index.reshape(-1), axis=0).reshape(index.shape + (BS,))
    live = (jnp.arange(K, dtype=jnp.int32)[None, None, :] < lives[:, :, None]).astype(
        jnp.float32
    )
    values = vals.reshape(vals.shape[:2] + (K, BS, BS))
    product = jnp.einsum("yxkij,yxkj,yxk->yxi", values, picked, live, precision=highest)
    product = product.reshape(3, span)
    coarse_product = product[:2].reshape(1, 2, span)

    pick = (2 * np.arange(nw)[:, None] + np.arange(3)[None, :]) % span
    back = jnp.transpose(product[:, pick], (1, 0, 2))
    got = lax.all_to_all(back, "wide", 0, 0, tiled=True)
    hx = jnp.stack([got[:, :, 0:2], got[:, :, 1:3]], axis=-1).reshape(nw, 3, 4)
    hy = jnp.stack([hx[:, 0:2], hx[:, 1:3]], axis=2).reshape(nw, 4, 4)
    hz = jnp.stack([hy, jnp.roll(hy, -1, axis=0)], axis=1).reshape(2 * nw, 4, 4)
    correction = jnp.transpose(hz, (2, 1, 0))
    for axis in range(3):
        correction = contract(correction, up_tables[axis], axis)
    second = first + correction
    smoothed = chebyshev(second, rhs_local, metric, helm, tables, inverse, None)
    return (smoothed, coarse_product)


def solution(mesh):
    placed = (
        P("wide", "deep", None),
        P(None, "wide", "deep", None),
        P("wide", "deep", None),
        P("wide", "deep", None, None),
        P("wide", "deep", None),
        P("wide", "deep", None, None),
    )
    return jax.shard_map(
        local,
        mesh=mesh,
        in_specs=placed,
        out_specs=(P("wide", "deep", None), P("wide", "deep", None)),
        check_vma=False,
    )
```

```python
import jax
import jax.numpy as jnp
import numpy as np
from jax import lax
from jax.sharding import PartitionSpec as P

NP = 8
K = 8
BS = 8


upper_bound = 6.0
lower_bound = 0.6
highest = lax.Precision.HIGHEST


def gll_tables(count):
    order = count - 1
    nodes = np.cos(np.pi * np.arange(count) / order)
    legendre = np.zeros((count, count))
    for sweep in range(101):
        legendre[:, 0] = 1.0
        legendre[:, 1] = nodes
        for degree in range(2, count):
            legendre[:, degree] = (
                (2 * degree - 1) * nodes * legendre[:, degree - 1]
                - (degree - 1) * legendre[:, degree - 2]
            ) / degree
        if sweep < 100:
            nodes = nodes - (nodes * legendre[:, order] - legendre[:, order - 1]) / (
                count * legendre[:, order]
            )
    nodes = nodes[::-1].copy()
    values = legendre[::-1, order].copy()
    identity_table = np.eye(count)
    spacing = nodes[:, None] - nodes[None, :] + identity_table
    derivative = values[:, None] / values[None, :] / spacing
    derivative = derivative * (1.0 - identity_table)
    derivative[0, 0] = -order * (order + 1) / 4.0
    derivative[-1, -1] = order * (order + 1) / 4.0
    linear = np.stack([(1.0 - nodes) / 2.0, (1.0 + nodes) / 2.0], axis=1)
    return (np.asarray(derivative, np.float32), np.asarray(linear, np.float32))


def block_extent():
    return 128


def repeat_table(small, copies):
    return jnp.asarray(np.kron(np.eye(copies, dtype=np.float32), small))


def contract(field, table, axis):
    if axis == 0:
        return jnp.einsum("mi,iyz->myz", table, field, precision=highest)
    if axis == 1:
        return jnp.einsum("mj,xjz->xmz", table, field, precision=highest)
    shape = field.shape
    blocked = table.shape[1]
    grid = field.reshape(shape[0], shape[1], shape[2] // blocked, blocked)
    result = jnp.einsum("mk,xynk->xynm", table, grid, precision=highest)
    return result.reshape(shape[0], shape[1], -1)


def shift(value, dw, dd):
    nw = lax.axis_size("wide")
    nd = lax.axis_size("deep")
    if dd == 0:
        pairs = [((w + dw) % nw, w) for w in range(nw)]
        return lax.ppermute(value, "wide", pairs)
    if dw == 0:
        pairs = [((d + dd) % nd, d) for d in range(nd)]
        return lax.ppermute(value, "deep", pairs)
    pairs = []
    for w in range(nw):
        for d in range(nd):
            src = ((w + dw) % nw) * nd + (d + dd) % nd
            pairs.append((src, w * nd + d))
    return lax.ppermute(value, ("wide", "deep"), pairs)


def node_mask(length, count, node, axis, ndim):
    index = lax.broadcasted_iota(jnp.int32, (length,), 0) % count == node
    shape = [1] * ndim
    shape[axis] = length
    return index.reshape(shape)


def assemble(field, count, carry=None):
    nd = field.ndim
    X, Y, Z = field.shape[-3:]
    lx = shift(field[..., -1, :, :], -1, 0)
    rx = shift(field[..., 0, :, :], 1, 0)
    ext = jnp.concatenate([lx[..., None, :, :], field, rx[..., None, :, :]], axis=-3)
    hi = node_mask(X, count, count - 1, nd - 3, nd)
    lo = node_mask(X, count, 0, nd - 3, nd)
    field = (
        ext[..., 1 : X + 1, :, :]
        + jnp.where(hi, ext[..., 2 : X + 2, :, :], 0.0)
        + jnp.where(lo, ext[..., 0:X, :, :], 0.0)
    )
    ly = shift(field[..., :, -1, :], 0, -1)
    face = field[..., :, 0, :]
    carried = None
    if carry is None:
        ry = shift(face, 0, 1)
    else:
        packed = shift(jnp.concatenate([face.reshape(-1), carry]), 0, 1)
        ry = packed[: face.size].reshape(face.shape)
        carried = packed[face.size :]
    ext = jnp.concatenate([ly[..., :, None, :], field, ry[..., :, None, :]], axis=-2)
    hi = node_mask(Y, count, count - 1, nd - 2, nd)
    lo = node_mask(Y, count, 0, nd - 2, nd)
    field = (
        ext[..., :, 1 : Y + 1, :]
        + jnp.where(hi, ext[..., :, 2 : Y + 2, :], 0.0)
        + jnp.where(lo, ext[..., :, 0:Y, :], 0.0)
    )
    hi = node_mask(Z, count, count - 1, nd - 1, nd)
    lo = node_mask(Z, count, 0, nd - 1, nd)
    field = (
        field
        + jnp.where(hi, jnp.roll(field, -1, axis=-1), 0.0)
        + jnp.where(lo, jnp.roll(field, 1, axis=-1), 0.0)
    )
    if carry is None:
        return field
    return field, carried


def apply_operator(field, metric, helm, tables):
    total = helm * field
    for axis in range(3):
        slope = contract(field, tables[axis], axis)
        total = total + contract(metric[axis] * slope, tables[axis].T, axis)
    return total


def chebyshev(solution, rhs_local, metric, helm, tables, inverse, first_residual):
    centre = (upper_bound + lower_bound) / 2.0
    half_width = (upper_bound - lower_bound) / 2.0
    aspect = centre / half_width
    weight_prev = 1.0 / aspect
    if first_residual is not None:
        residual = first_residual
    else:
        residual = assemble(rhs_local - apply_operator(solution, metric, helm, tables), NP)
    update = inverse * residual / centre
    solution = solution + update
    residual = assemble(rhs_local - apply_operator(solution, metric, helm, tables), NP)
    weight_next = 1.0 / (2.0 * aspect - weight_prev)
    update = (
        weight_next * weight_prev * update + 2.0 * weight_next / half_width * inverse * residual
    )
    solution = solution + update
    return solution


def body(rhs_local, metric, helm, columns, live_blocks, block_values):
    derivative, linear = gll_tables(NP)
    shape = rhs_local.shape
    nw = lax.axis_size("wide")
    copies = (shape[0] // NP, shape[1] // NP, block_extent() // NP)
    tables = tuple((repeat_table(derivative, copies[axis]) for axis in range(3)))
    square_tables = tuple(
        (repeat_table(derivative * derivative, copies[axis]) for axis in range(3))
    )
    down_tables = tuple((repeat_table(linear.T, copies[axis]) for axis in range(3)))
    up_tables = tuple((repeat_table(linear, copies[axis]) for axis in range(3)))

    diagonal = helm
    for axis in range(3):
        diagonal = diagonal + contract(metric[axis], square_tables[axis].T, axis)
    nw_ = lax.axis_size("wide")
    nxb_ = columns.shape[2]
    xbs_ = np.stack([(2 * np.arange(nw_) + 2 * j) // BS % nxb_ for j in range(2)], axis=1)
    packed = jnp.concatenate(
        [
            block_values[0],
            columns[0].astype(jnp.float32),
            live_blocks[0].astype(jnp.float32)[..., None],
        ],
        axis=-1,
    )
    packed = jnp.transpose(jnp.take(packed, jnp.asarray(xbs_), axis=1), (1, 0, 2, 3))
    fetched = lax.all_to_all(packed, "wide", 0, 0, tiled=True)
    fetched = jnp.concatenate([fetched, shift(fetched[:, :1], 0, 1)], axis=1)
    nvals = block_values.shape[3]
    fetched_vals = fetched[..., :nvals]
    fetched_cols = fetched[..., nvals : nvals + K].astype(jnp.int32)
    fetched_live = fetched[..., nvals + K].astype(jnp.int32)
    both = assemble(jnp.stack([diagonal, rhs_local]), NP)
    inverse = 1.0 / both[0]
    first = chebyshev(
        jnp.zeros_like(rhs_local), rhs_local, metric, helm, tables, inverse, both[1]
    )
    local_res = rhs_local - apply_operator(first, metric, helm, tables)
    corners = local_res
    for axis in range(3):
        corners = contract(corners, down_tables[axis], axis)

    cx, cy, _ = corners.shape
    ext = jnp.concatenate([shift(corners, 0, -1), corners, shift(corners, 0, 1)], axis=1)
    qz = ext[:, :, 0::2] + jnp.roll(ext, 1, axis=2)[:, :, 0::2]
    qy = qz[:, cy : cy + 7 : 2] + qz[:, cy - 1 : cy + 6 : 2]
    zero = jnp.zeros_like(qy[:1])
    qx = jnp.concatenate([zero, qy, zero], axis=0)
    partial = qx[1 : cx + 2 : 2] + qx[0 : cx + 1 : 2]

    got = lax.all_to_all(
        jnp.broadcast_to(partial[None], (nw,) + partial.shape), "wide", 0, 0, tiled=True
    )
    even = got[:, 0] + jnp.roll(got[:, 2], 1, axis=0)
    got = jnp.stack([even, got[:, 1]], axis=1)
    layers = got.shape[-1]
    frame = jnp.transpose(got, (3, 2, 0, 1)).reshape(layers, 4, -1)
    span = frame.shape[2]
    nxb = span // BS
    frame_rows = frame.reshape(-1, BS)
    w_index = lax.axis_index("wide")

    def rows_of(cols, lives, vals, z, y_off):
        layer = cols // (2 * nxb)
        block = cols % (2 * nxb)
        src = (z + layer - 1) % layers
        index = ((src * 4 + y_off + block // nxb) * nxb + block % nxb)
        picked = jnp.take(frame_rows, index.reshape(-1), axis=0).reshape(index.shape + (BS,))
        live = (jnp.arange(K, dtype=jnp.int32) < lives[..., None]).astype(jnp.float32)
        values = vals.reshape(vals.shape[:-1] + (K, BS, BS))
        return jnp.einsum("...kij,...kj,...k->...i", values, picked, live, precision=highest)

    own = rows_of(columns[0], live_blocks[0], block_values[0], w_index, 0)
    coarse_product = own.reshape(1, 2, span)

    corr = rows_of(
        fetched_cols,
        fetched_live,
        fetched_vals,
        jnp.arange(layers, dtype=jnp.int32)[:, None, None, None],
        jnp.array([0, 0, 2], jnp.int32)[None, :, None, None],
    )
    corr = corr.reshape(layers, 3, 2 * BS)
    x_need = (2 * w_index + jnp.arange(3, dtype=jnp.int32)) % span
    first_block = (2 * w_index // BS) % nxb
    virtual = jnp.where(x_need // BS == first_block, 0, BS) + x_need % BS
    got = jnp.take(corr, virtual, axis=2)
    hx = jnp.stack([got[:, :, 0:2], got[:, :, 1:3]], axis=-1).reshape(nw, 3, 4)
    hy = jnp.stack([hx[:, 0:2], hx[:, 1:3]], axis=2).reshape(nw, 4, 4)
    hz = jnp.stack([hy, jnp.roll(hy, -1, axis=0)], axis=1).reshape(2 * nw, 4, 4)
    correction = jnp.transpose(hz, (2, 1, 0))
    for axis in range(3):
        correction = contract(correction, up_tables[axis], axis)
    second = first + correction
    smoothed = chebyshev(second, rhs_local, metric, helm, tables, inverse, None)
    return (smoothed, coarse_product)


def solution(mesh):
    placed = (
        P("wide", "deep", None),
        P(None, "wide", "deep", None),
        P("wide", "deep", None),
        P("wide", "deep", None, None),
        P("wide", "deep", None),
        P("wide", "deep", None, None),
    )
    return jax.shard_map(
        body,
        mesh=mesh,
        in_specs=placed,
        out_specs=(P("wide", "deep", None), P("wide", "deep", None)),
        check_vma=False,
    )
```

```python
import jax
import jax.numpy as jnp
import numpy as np
from jax import lax
from jax.sharding import PartitionSpec as P

NP = 8
K = 8
BS = 8


upper_bound = 6.0
lower_bound = 0.6
highest = lax.Precision.HIGHEST


def gll_tables(count):
    order = count - 1
    nodes = np.cos(np.pi * np.arange(count) / order)
    legendre = np.zeros((count, count))
    for sweep in range(101):
        legendre[:, 0] = 1.0
        legendre[:, 1] = nodes
        for degree in range(2, count):
            legendre[:, degree] = (
                (2 * degree - 1) * nodes * legendre[:, degree - 1]
                - (degree - 1) * legendre[:, degree - 2]
            ) / degree
        if sweep < 100:
            nodes = nodes - (nodes * legendre[:, order] - legendre[:, order - 1]) / (
                count * legendre[:, order]
            )
    nodes = nodes[::-1].copy()
    values = legendre[::-1, order].copy()
    identity_table = np.eye(count)
    spacing = nodes[:, None] - nodes[None, :] + identity_table
    derivative = values[:, None] / values[None, :] / spacing
    derivative = derivative * (1.0 - identity_table)
    derivative[0, 0] = -order * (order + 1) / 4.0
    derivative[-1, -1] = order * (order + 1) / 4.0
    linear = np.stack([(1.0 - nodes) / 2.0, (1.0 + nodes) / 2.0], axis=1)
    return (np.asarray(derivative, np.float32), np.asarray(linear, np.float32))


def block_extent():
    return 128


def repeat_table(small, copies):
    return jnp.asarray(np.kron(np.eye(copies, dtype=np.float32), small))


def contract(field, table, axis):
    if axis == 0:
        return jnp.einsum("mi,iyz->myz", table, field, precision=highest)
    if axis == 1:
        return jnp.einsum("mj,xjz->xmz", table, field, precision=highest)
    shape = field.shape
    blocked = table.shape[1]
    grid = field.reshape(shape[0], shape[1], shape[2] // blocked, blocked)
    result = jnp.einsum("mk,xynk->xynm", table, grid, precision=highest)
    return result.reshape(shape[0], shape[1], -1)


def shift(value, dw, dd):
    nw = lax.axis_size("wide")
    nd = lax.axis_size("deep")
    if dd == 0:
        pairs = [((w + dw) % nw, w) for w in range(nw)]
        return lax.ppermute(value, "wide", pairs)
    if dw == 0:
        pairs = [((d + dd) % nd, d) for d in range(nd)]
        return lax.ppermute(value, "deep", pairs)
    pairs = []
    for w in range(nw):
        for d in range(nd):
            src = ((w + dw) % nw) * nd + (d + dd) % nd
            pairs.append((src, w * nd + d))
    return lax.ppermute(value, ("wide", "deep"), pairs)


def node_mask(length, count, node, axis, ndim):
    index = lax.broadcasted_iota(jnp.int32, (length,), 0) % count == node
    shape = [1] * ndim
    shape[axis] = length
    return index.reshape(shape)


def assemble(field, count, carry=None):
    nd = field.ndim
    X, Y, Z = field.shape[-3:]
    lx = shift(field[..., -1, :, :], -1, 0)
    rx = shift(field[..., 0, :, :], 1, 0)
    ext = jnp.concatenate([lx[..., None, :, :], field, rx[..., None, :, :]], axis=-3)
    hi = node_mask(X, count, count - 1, nd - 3, nd)
    lo = node_mask(X, count, 0, nd - 3, nd)
    field = (
        ext[..., 1 : X + 1, :, :]
        + jnp.where(hi, ext[..., 2 : X + 2, :, :], 0.0)
        + jnp.where(lo, ext[..., 0:X, :, :], 0.0)
    )
    ly = shift(field[..., :, -1, :], 0, -1)
    face = field[..., :, 0, :]
    carried = None
    if carry is None:
        ry = shift(face, 0, 1)
    else:
        packed = shift(jnp.concatenate([face.reshape(-1), carry]), 0, 1)
        ry = packed[: face.size].reshape(face.shape)
        carried = packed[face.size :]
    ext = jnp.concatenate([ly[..., :, None, :], field, ry[..., :, None, :]], axis=-2)
    hi = node_mask(Y, count, count - 1, nd - 2, nd)
    lo = node_mask(Y, count, 0, nd - 2, nd)
    field = (
        ext[..., :, 1 : Y + 1, :]
        + jnp.where(hi, ext[..., :, 2 : Y + 2, :], 0.0)
        + jnp.where(lo, ext[..., :, 0:Y, :], 0.0)
    )
    hi = node_mask(Z, count, count - 1, nd - 1, nd)
    lo = node_mask(Z, count, 0, nd - 1, nd)
    field = (
        field
        + jnp.where(hi, jnp.roll(field, -1, axis=-1), 0.0)
        + jnp.where(lo, jnp.roll(field, 1, axis=-1), 0.0)
    )
    if carry is None:
        return field
    return field, carried


def apply_operator(field, metric, helm, tables):
    shape = field.shape
    flat = field.reshape(-1, shape[-1])
    total = helm.reshape(flat.shape) * flat
    tx, ty, tz = tables
    for axis, table in ((0, tx), (1, ty)):
        slope = jnp.dot(table, flat, precision=highest)
        weighted = metric[axis].reshape(flat.shape) * slope
        total = total + jnp.dot(table.T, weighted, precision=highest)
    slope = jnp.dot(flat, tz.T, precision=highest)
    weighted = metric[2].reshape(flat.shape) * slope
    total = total + jnp.dot(weighted, tz, precision=highest)
    return total.reshape(shape)


def big_tables(small, shape):
    X, Y, Z = shape
    n = small.shape[0]
    px = np.kron(np.kron(np.eye(X // n, dtype=np.float32), small), np.eye(Y, dtype=np.float32))
    py = np.kron(np.eye(X, dtype=np.float32), np.kron(np.eye(Y // n, dtype=np.float32), small))
    pz = np.kron(np.eye(Z // n, dtype=np.float32), small)
    return tuple(jnp.asarray(t) for t in (px, py, pz))


def chebyshev(solution, rhs_local, metric, helm, tables, inverse, first_residual):
    centre = (upper_bound + lower_bound) / 2.0
    half_width = (upper_bound - lower_bound) / 2.0
    aspect = centre / half_width
    weight_prev = 1.0 / aspect
    if first_residual is not None:
        residual = first_residual
    else:
        residual = assemble(rhs_local - apply_operator(solution, metric, helm, tables), NP)
    update = inverse * residual / centre
    solution = solution + update
    residual = assemble(rhs_local - apply_operator(solution, metric, helm, tables), NP)
    weight_next = 1.0 / (2.0 * aspect - weight_prev)
    update = (
        weight_next * weight_prev * update + 2.0 * weight_next / half_width * inverse * residual
    )
    solution = solution + update
    return solution


def local(rhs_local, metric, helm, columns, live_blocks, block_values):
    derivative, linear = gll_tables(NP)
    shape = rhs_local.shape
    nw = lax.axis_size("wide")
    copies = (shape[0] // NP, shape[1] // NP, block_extent() // NP)
    tables = big_tables(derivative, shape)
    sx, sy, sz = big_tables(derivative * derivative, shape)
    down_tables = tuple((repeat_table(linear.T, copies[axis]) for axis in range(3)))
    up_tables = tuple((repeat_table(linear, copies[axis]) for axis in range(3)))

    rows = shape[0] * shape[1]
    diagonal = (
        helm.reshape(rows, -1)
        + jnp.dot(sx.T, metric[0].reshape(rows, -1), precision=highest)
        + jnp.dot(sy.T, metric[1].reshape(rows, -1), precision=highest)
        + jnp.dot(metric[2].reshape(rows, -1), sz, precision=highest)
    ).reshape(shape)
    mats = jnp.concatenate(
        [
            block_values[0, 0].reshape(-1),
            columns[0, 0].astype(jnp.float32).reshape(-1),
            live_blocks[0, 0].astype(jnp.float32),
        ]
    )
    both, mats = assemble(jnp.stack([diagonal, rhs_local]), NP, mats)
    nvals = block_values.shape[2] * block_values.shape[3]
    ncols = columns.shape[2] * columns.shape[3]
    next_values = mats[:nvals].reshape(block_values.shape[2:])
    next_columns = mats[nvals : nvals + ncols].astype(jnp.int32).reshape(columns.shape[2:])
    next_live = mats[nvals + ncols :].astype(jnp.int32)
    inverse = 1.0 / both[0]
    first = chebyshev(
        jnp.zeros_like(rhs_local), rhs_local, metric, helm, tables, inverse, both[1]
    )
    local_res = rhs_local - apply_operator(first, metric, helm, tables)
    corners = local_res
    for axis in range(3):
        corners = contract(corners, down_tables[axis], axis)

    cx, cy, cz = corners.shape
    ext = jnp.concatenate([shift(corners, 0, -1), corners, shift(corners, 0, 1)], axis=1)
    qz = ext[:, :, 0::2] + jnp.roll(ext, 1, axis=2)[:, :, 0::2]
    qy = qz[:, cy : cy + 7 : 2] + qz[:, cy - 1 : cy + 6 : 2]
    zero = jnp.zeros_like(qy[:1])
    qx = jnp.concatenate([zero, qy, zero], axis=0)
    partial = qx[1 : cx + 2 : 2] + qx[0 : cx + 1 : 2]

    sent = jnp.stack(
        [jnp.roll(partial, 1, axis=2), partial, jnp.roll(partial, -1, axis=2)], axis=-1
    )
    sent = jnp.transpose(sent, (2, 0, 1, 3))
    got = lax.all_to_all(sent, "wide", 0, 0, tiled=True)
    even = got[:, 0] + jnp.roll(got[:, 2], 1, axis=0)
    got = jnp.stack([even, got[:, 1]], axis=1)
    frame = jnp.transpose(got, (3, 2, 0, 1)).reshape(3, 4, -1)
    span = frame.shape[2]
    nxb = span // BS
    frame_rows = frame.reshape(-1, BS)

    cols = jnp.concatenate([columns[0], next_columns[None]], axis=0)
    lives = jnp.concatenate([live_blocks[0], next_live[None]], axis=0)
    vals = jnp.concatenate([block_values[0], next_values[None]], axis=0)
    y_off = jnp.array([0, 0, 2], jnp.int32)[:, None, None]
    layer = cols // (2 * nxb)
    block = cols % (2 * nxb)
    index = (layer * 4 + y_off + block // nxb) * nxb + block % nxb
    picked = jnp.take(frame_rows, index.reshape(-1), axis=0).reshape(index.shape + (BS,))
    live = (jnp.arange(K, dtype=jnp.int32)[None, None, :] < lives[:, :, None]).astype(
        jnp.float32
    )
    values = vals.reshape(vals.shape[:2] + (K, BS, BS))
    product = jnp.einsum("yxkij,yxkj,yxk->yxi", values, picked, live, precision=highest)
    product = product.reshape(3, span)
    coarse_product = product[:2].reshape(1, 2, span)

    pick = (2 * np.arange(nw)[:, None] + np.arange(3)[None, :]) % span
    back = jnp.transpose(product[:, pick], (1, 0, 2))
    got = lax.all_to_all(back, "wide", 0, 0, tiled=True)
    hx = jnp.stack([got[:, :, 0:2], got[:, :, 1:3]], axis=-1).reshape(nw, 3, 4)
    hy = jnp.stack([hx[:, 0:2], hx[:, 1:3]], axis=2).reshape(nw, 4, 4)
    hz = jnp.stack([hy, jnp.roll(hy, -1, axis=0)], axis=1).reshape(2 * nw, 4, 4)
    correction = jnp.transpose(hz, (2, 1, 0))
    for axis in range(3):
        correction = contract(correction, up_tables[axis], axis)
    second = first + correction
    smoothed = chebyshev(second, rhs_local, metric, helm, tables, inverse, None)
    return (smoothed, coarse_product)


def solution(mesh):
    placed = (
        P("wide", "deep", None),
        P(None, "wide", "deep", None),
        P("wide", "deep", None),
        P("wide", "deep", None, None),
        P("wide", "deep", None),
        P("wide", "deep", None, None),
    )
    return jax.shard_map(
        local,
        mesh=mesh,
        in_specs=placed,
        out_specs=(P("wide", "deep", None), P("wide", "deep", None)),
        check_vma=False,
    )
```

```python
import jax
import jax.numpy as jnp
import numpy as np
from jax import lax
from jax.sharding import PartitionSpec as P

NP = 8
K = 8
BS = 8


upper_bound = 6.0
lower_bound = 0.6
highest = lax.Precision.HIGHEST
fast = lax.Precision.HIGH


def gll_tables(count):
    order = count - 1
    nodes = np.cos(np.pi * np.arange(count) / order)
    legendre = np.zeros((count, count))
    for sweep in range(101):
        legendre[:, 0] = 1.0
        legendre[:, 1] = nodes
        for degree in range(2, count):
            legendre[:, degree] = (
                (2 * degree - 1) * nodes * legendre[:, degree - 1]
                - (degree - 1) * legendre[:, degree - 2]
            ) / degree
        if sweep < 100:
            nodes = nodes - (nodes * legendre[:, order] - legendre[:, order - 1]) / (
                count * legendre[:, order]
            )
    nodes = nodes[::-1].copy()
    values = legendre[::-1, order].copy()
    identity_table = np.eye(count)
    spacing = nodes[:, None] - nodes[None, :] + identity_table
    derivative = values[:, None] / values[None, :] / spacing
    derivative = derivative * (1.0 - identity_table)
    derivative[0, 0] = -order * (order + 1) / 4.0
    derivative[-1, -1] = order * (order + 1) / 4.0
    linear = np.stack([(1.0 - nodes) / 2.0, (1.0 + nodes) / 2.0], axis=1)
    return (np.asarray(derivative, np.float32), np.asarray(linear, np.float32))


def block_extent():
    return 128


def repeat_table(small, copies):
    return jnp.asarray(np.kron(np.eye(copies, dtype=np.float32), small))


def contract(field, table, axis):
    if axis == 0:
        return jnp.einsum("mi,iyz->myz", table, field, precision=highest)
    if axis == 1:
        return jnp.einsum("mj,xjz->xmz", table, field, precision=highest)
    shape = field.shape
    blocked = table.shape[1]
    grid = field.reshape(shape[0], shape[1], shape[2] // blocked, blocked)
    result = jnp.einsum("mk,xynk->xynm", table, grid, precision=highest)
    return result.reshape(shape[0], shape[1], -1)


def shift(value, dw, dd):
    nw = lax.axis_size("wide")
    nd = lax.axis_size("deep")
    if dd == 0:
        pairs = [((w + dw) % nw, w) for w in range(nw)]
        return lax.ppermute(value, "wide", pairs)
    if dw == 0:
        pairs = [((d + dd) % nd, d) for d in range(nd)]
        return lax.ppermute(value, "deep", pairs)
    pairs = []
    for w in range(nw):
        for d in range(nd):
            src = ((w + dw) % nw) * nd + (d + dd) % nd
            pairs.append((src, w * nd + d))
    return lax.ppermute(value, ("wide", "deep"), pairs)


def node_mask(length, count, node, axis, ndim):
    index = lax.broadcasted_iota(jnp.int32, (length,), 0) % count == node
    shape = [1] * ndim
    shape[axis] = length
    return index.reshape(shape)


def assemble(field, count, carry=None):
    nd = field.ndim
    X, Y, Z = field.shape[-3:]
    lx = shift(field[..., -1, :, :], -1, 0)
    rx = shift(field[..., 0, :, :], 1, 0)
    ext = jnp.concatenate([lx[..., None, :, :], field, rx[..., None, :, :]], axis=-3)
    hi = node_mask(X, count, count - 1, nd - 3, nd)
    lo = node_mask(X, count, 0, nd - 3, nd)
    field = (
        ext[..., 1 : X + 1, :, :]
        + jnp.where(hi, ext[..., 2 : X + 2, :, :], 0.0)
        + jnp.where(lo, ext[..., 0:X, :, :], 0.0)
    )
    ly = shift(field[..., :, -1, :], 0, -1)
    face = field[..., :, 0, :]
    carried = None
    if carry is None:
        ry = shift(face, 0, 1)
    else:
        packed = shift(jnp.concatenate([face.reshape(-1), carry]), 0, 1)
        ry = packed[: face.size].reshape(face.shape)
        carried = packed[face.size :]
    ext = jnp.concatenate([ly[..., :, None, :], field, ry[..., :, None, :]], axis=-2)
    hi = node_mask(Y, count, count - 1, nd - 2, nd)
    lo = node_mask(Y, count, 0, nd - 2, nd)
    field = (
        ext[..., :, 1 : Y + 1, :]
        + jnp.where(hi, ext[..., :, 2 : Y + 2, :], 0.0)
        + jnp.where(lo, ext[..., :, 0:Y, :], 0.0)
    )
    hi = node_mask(Z, count, count - 1, nd - 1, nd)
    lo = node_mask(Z, count, 0, nd - 1, nd)
    field = (
        field
        + jnp.where(hi, jnp.roll(field, -1, axis=-1), 0.0)
        + jnp.where(lo, jnp.roll(field, 1, axis=-1), 0.0)
    )
    if carry is None:
        return field
    return field, carried


def apply_operator(field, metric, helm, tables):
    shape = field.shape
    flat = field.reshape(-1, shape[-1])
    total = helm.reshape(flat.shape) * flat
    tx, ty, tz = tables
    for axis, table in ((0, tx), (1, ty)):
        slope = jnp.dot(table, flat, precision=fast)
        weighted = metric[axis].reshape(flat.shape) * slope
        total = total + jnp.dot(table.T, weighted, precision=fast)
    slope = jnp.dot(flat, tz.T, precision=fast)
    weighted = metric[2].reshape(flat.shape) * slope
    total = total + jnp.dot(weighted, tz, precision=fast)
    return total.reshape(shape)


def big_tables(small, shape):
    X, Y, Z = shape
    n = small.shape[0]
    px = np.kron(np.kron(np.eye(X // n, dtype=np.float32), small), np.eye(Y, dtype=np.float32))
    py = np.kron(np.eye(X, dtype=np.float32), np.kron(np.eye(Y // n, dtype=np.float32), small))
    pz = np.kron(np.eye(Z // n, dtype=np.float32), small)
    return tuple(jnp.asarray(t) for t in (px, py, pz))


def chebyshev(solution, rhs_local, metric, helm, tables, inverse, first_residual):
    centre = (upper_bound + lower_bound) / 2.0
    half_width = (upper_bound - lower_bound) / 2.0
    aspect = centre / half_width
    weight_prev = 1.0 / aspect
    if first_residual is not None:
        residual = first_residual
    else:
        residual = assemble(rhs_local - apply_operator(solution, metric, helm, tables), NP)
    update = inverse * residual / centre
    solution = solution + update
    residual = assemble(rhs_local - apply_operator(solution, metric, helm, tables), NP)
    weight_next = 1.0 / (2.0 * aspect - weight_prev)
    update = (
        weight_next * weight_prev * update + 2.0 * weight_next / half_width * inverse * residual
    )
    solution = solution + update
    return solution


def local(rhs_local, metric, helm, columns, live_blocks, block_values):
    derivative, linear = gll_tables(NP)
    shape = rhs_local.shape
    nw = lax.axis_size("wide")
    copies = (shape[0] // NP, shape[1] // NP, block_extent() // NP)
    tables = big_tables(derivative, shape)
    sx, sy, sz = big_tables(derivative * derivative, shape)
    down_tables = tuple((repeat_table(linear.T, copies[axis]) for axis in range(3)))
    up_tables = tuple((repeat_table(linear, copies[axis]) for axis in range(3)))

    rows = shape[0] * shape[1]
    diagonal = (
        helm.reshape(rows, -1)
        + jnp.dot(sx.T, metric[0].reshape(rows, -1), precision=fast)
        + jnp.dot(sy.T, metric[1].reshape(rows, -1), precision=fast)
        + jnp.dot(metric[2].reshape(rows, -1), sz, precision=fast)
    ).reshape(shape)
    mats = jnp.concatenate(
        [
            block_values[0, 0].reshape(-1),
            columns[0, 0].astype(jnp.float32).reshape(-1),
            live_blocks[0, 0].astype(jnp.float32),
        ]
    )
    both, mats = assemble(jnp.stack([diagonal, rhs_local]), NP, mats)
    nvals = block_values.shape[2] * block_values.shape[3]
    ncols = columns.shape[2] * columns.shape[3]
    next_values = mats[:nvals].reshape(block_values.shape[2:])
    next_columns = mats[nvals : nvals + ncols].astype(jnp.int32).reshape(columns.shape[2:])
    next_live = mats[nvals + ncols :].astype(jnp.int32)
    inverse = 1.0 / both[0]
    first = chebyshev(
        jnp.zeros_like(rhs_local), rhs_local, metric, helm, tables, inverse, both[1]
    )
    local_res = rhs_local - apply_operator(first, metric, helm, tables)
    corners = local_res
    for axis in range(3):
        corners = contract(corners, down_tables[axis], axis)

    cx, cy, cz = corners.shape
    ext = jnp.concatenate([shift(corners, 0, -1), corners, shift(corners, 0, 1)], axis=1)
    qz = ext[:, :, 0::2] + jnp.roll(ext, 1, axis=2)[:, :, 0::2]
    qy = qz[:, cy : cy + 7 : 2] + qz[:, cy - 1 : cy + 6 : 2]
    zero = jnp.zeros_like(qy[:1])
    qx = jnp.concatenate([zero, qy, zero], axis=0)
    partial = qx[1 : cx + 2 : 2] + qx[0 : cx + 1 : 2]

    sent = jnp.stack(
        [jnp.roll(partial, 1, axis=2), partial, jnp.roll(partial, -1, axis=2)], axis=-1
    )
    sent = jnp.transpose(sent, (2, 0, 1, 3))
    got = lax.all_to_all(sent, "wide", 0, 0, tiled=True)
    even = got[:, 0] + jnp.roll(got[:, 2], 1, axis=0)
    got = jnp.stack([even, got[:, 1]], axis=1)
    frame = jnp.transpose(got, (3, 2, 0, 1)).reshape(3, 4, -1)
    span = frame.shape[2]
    nxb = span // BS
    frame_rows = frame.reshape(-1, BS)

    cols = jnp.concatenate([columns[0], next_columns[None]], axis=0)
    lives = jnp.concatenate([live_blocks[0], next_live[None]], axis=0)
    vals = jnp.concatenate([block_values[0], next_values[None]], axis=0)
    y_off = jnp.array([0, 0, 2], jnp.int32)[:, None, None]
    layer = cols // (2 * nxb)
    block = cols % (2 * nxb)
    index = (layer * 4 + y_off + block // nxb) * nxb + block % nxb
    picked = jnp.take(frame_rows, index.reshape(-1), axis=0).reshape(index.shape + (BS,))
    live = (jnp.arange(K, dtype=jnp.int32)[None, None, :] < lives[:, :, None]).astype(
        jnp.float32
    )
    values = vals.reshape(vals.shape[:2] + (K, BS, BS))
    product = jnp.einsum("yxkij,yxkj,yxk->yxi", values, picked, live, precision=highest)
    product = product.reshape(3, span)
    coarse_product = product[:2].reshape(1, 2, span)

    pick = (2 * np.arange(nw)[:, None] + np.arange(3)[None, :]) % span
    back = jnp.transpose(product[:, pick], (1, 0, 2))
    got = lax.all_to_all(back, "wide", 0, 0, tiled=True)
    hx = jnp.stack([got[:, :, 0:2], got[:, :, 1:3]], axis=-1).reshape(nw, 3, 4)
    hy = jnp.stack([hx[:, 0:2], hx[:, 1:3]], axis=2).reshape(nw, 4, 4)
    hz = jnp.stack([hy, jnp.roll(hy, -1, axis=0)], axis=1).reshape(2 * nw, 4, 4)
    correction = jnp.transpose(hz, (2, 1, 0))
    for axis in range(3):
        correction = contract(correction, up_tables[axis], axis)
    second = first + correction
    smoothed = chebyshev(second, rhs_local, metric, helm, tables, inverse, None)
    return (smoothed, coarse_product)


def solution(mesh):
    placed = (
        P("wide", "deep", None),
        P(None, "wide", "deep", None),
        P("wide", "deep", None),
        P("wide", "deep", None, None),
        P("wide", "deep", None),
        P("wide", "deep", None, None),
    )
    return jax.shard_map(
        local,
        mesh=mesh,
        in_specs=placed,
        out_specs=(P("wide", "deep", None), P("wide", "deep", None)),
        check_vma=False,
    )
```

```python
import jax
import jax.numpy as jnp
import numpy as np
from jax import lax
from jax.sharding import PartitionSpec as P

NP = 8
K = 8
BS = 8


upper_bound = 6.0
lower_bound = 0.6
highest = lax.Precision.HIGHEST
fast = lax.Precision.HIGH


def gll_tables(count):
    order = count - 1
    nodes = np.cos(np.pi * np.arange(count) / order)
    legendre = np.zeros((count, count))
    for sweep in range(101):
        legendre[:, 0] = 1.0
        legendre[:, 1] = nodes
        for degree in range(2, count):
            legendre[:, degree] = (
                (2 * degree - 1) * nodes * legendre[:, degree - 1]
                - (degree - 1) * legendre[:, degree - 2]
            ) / degree
        if sweep < 100:
            nodes = nodes - (nodes * legendre[:, order] - legendre[:, order - 1]) / (
                count * legendre[:, order]
            )
    nodes = nodes[::-1].copy()
    values = legendre[::-1, order].copy()
    identity_table = np.eye(count)
    spacing = nodes[:, None] - nodes[None, :] + identity_table
    derivative = values[:, None] / values[None, :] / spacing
    derivative = derivative * (1.0 - identity_table)
    derivative[0, 0] = -order * (order + 1) / 4.0
    derivative[-1, -1] = order * (order + 1) / 4.0
    linear = np.stack([(1.0 - nodes) / 2.0, (1.0 + nodes) / 2.0], axis=1)
    return (np.asarray(derivative, np.float32), np.asarray(linear, np.float32))


def block_extent():
    return 128


def repeat_table(small, copies):
    return jnp.asarray(np.kron(np.eye(copies, dtype=np.float32), small))


def contract(field, table, axis):
    if axis == 0:
        return jnp.einsum("mi,iyz->myz", table, field, precision=highest)
    if axis == 1:
        return jnp.einsum("mj,xjz->xmz", table, field, precision=highest)
    shape = field.shape
    blocked = table.shape[1]
    grid = field.reshape(shape[0], shape[1], shape[2] // blocked, blocked)
    result = jnp.einsum("mk,xynk->xynm", table, grid, precision=highest)
    return result.reshape(shape[0], shape[1], -1)


def shift(value, dw, dd):
    nw = lax.axis_size("wide")
    nd = lax.axis_size("deep")
    if dd == 0:
        pairs = [((w + dw) % nw, w) for w in range(nw)]
        return lax.ppermute(value, "wide", pairs)
    if dw == 0:
        pairs = [((d + dd) % nd, d) for d in range(nd)]
        return lax.ppermute(value, "deep", pairs)
    pairs = []
    for w in range(nw):
        for d in range(nd):
            src = ((w + dw) % nw) * nd + (d + dd) % nd
            pairs.append((src, w * nd + d))
    return lax.ppermute(value, ("wide", "deep"), pairs)


def node_mask(length, count, node, axis, ndim):
    index = lax.broadcasted_iota(jnp.int32, (length,), 0) % count == node
    shape = [1] * ndim
    shape[axis] = length
    return index.reshape(shape)


def assemble(field, count, carry=None, faces=None):
    nd = field.ndim
    X, Y, Z = field.shape[-3:]
    low, high = (field[..., 0, :, :], field[..., -1, :, :]) if faces is None else faces
    lx = shift(high, -1, 0)
    rx = shift(low, 1, 0)
    ext = jnp.concatenate([lx[..., None, :, :], field, rx[..., None, :, :]], axis=-3)
    hi = node_mask(X, count, count - 1, nd - 3, nd)
    lo = node_mask(X, count, 0, nd - 3, nd)
    field = (
        ext[..., 1 : X + 1, :, :]
        + jnp.where(hi, ext[..., 2 : X + 2, :, :], 0.0)
        + jnp.where(lo, ext[..., 0:X, :, :], 0.0)
    )
    ly = shift(field[..., :, -1, :], 0, -1)
    face = field[..., :, 0, :]
    carried = None
    if carry is None:
        ry = shift(face, 0, 1)
    else:
        packed = shift(jnp.concatenate([face.reshape(-1), carry]), 0, 1)
        ry = packed[: face.size].reshape(face.shape)
        carried = packed[face.size :]
    ext = jnp.concatenate([ly[..., :, None, :], field, ry[..., :, None, :]], axis=-2)
    hi = node_mask(Y, count, count - 1, nd - 2, nd)
    lo = node_mask(Y, count, 0, nd - 2, nd)
    field = (
        ext[..., :, 1 : Y + 1, :]
        + jnp.where(hi, ext[..., :, 2 : Y + 2, :], 0.0)
        + jnp.where(lo, ext[..., :, 0:Y, :], 0.0)
    )
    hi = node_mask(Z, count, count - 1, nd - 1, nd)
    lo = node_mask(Z, count, 0, nd - 1, nd)
    field = (
        field
        + jnp.where(hi, jnp.roll(field, -1, axis=-1), 0.0)
        + jnp.where(lo, jnp.roll(field, 1, axis=-1), 0.0)
    )
    if carry is None:
        return field
    return field, carried


def apply_operator(field, metric, helm, tables):
    shape = field.shape
    flat = field.reshape(-1, shape[-1])
    total = helm.reshape(flat.shape) * flat
    tx, ty, tz = tables[:3]
    for axis, table in ((0, tx), (1, ty)):
        slope = jnp.dot(table, flat, precision=fast)
        weighted = metric[axis].reshape(flat.shape) * slope
        total = total + jnp.dot(table.T, weighted, precision=fast)
    slope = jnp.dot(flat, tz.T, precision=fast)
    weighted = metric[2].reshape(flat.shape) * slope
    total = total + jnp.dot(weighted, tz, precision=fast)
    return total.reshape(shape)


def operator_faces(field, metric, helm, tables, face_y):
    X, Y, Z = field.shape
    flat = field.reshape(X * Y, Z)
    tx, ty, tz = tables

    def planes(a):
        a = a.reshape(X * Y, -1)
        return jnp.concatenate([a[:Y], a[-Y:]], axis=0)

    slope = jnp.dot(tx, flat, precision=fast)
    weighted = metric[0].reshape(flat.shape) * slope
    total = jnp.dot(planes(tx.T), weighted, precision=fast)
    face = planes(field)
    total = total + planes(helm) * face
    slope = jnp.dot(face_y, face, precision=fast)
    total = total + jnp.dot(face_y.T, planes(metric[1]) * slope, precision=fast)
    slope = jnp.dot(face, tz.T, precision=fast)
    total = total + jnp.dot(planes(metric[2]) * slope, tz, precision=fast)
    return total


def big_tables(small, shape):
    X, Y, Z = shape
    n = small.shape[0]
    px = np.kron(np.kron(np.eye(X // n, dtype=np.float32), small), np.eye(Y, dtype=np.float32))
    py = np.kron(np.eye(X, dtype=np.float32), np.kron(np.eye(Y // n, dtype=np.float32), small))
    pz = np.kron(np.eye(Z // n, dtype=np.float32), small)
    return tuple(jnp.asarray(t) for t in (px, py, pz))


def residual_of(solution, rhs_local, metric, helm, tables):
    X, Y, Z = solution.shape
    full = rhs_local - apply_operator(solution, metric, helm, tables)
    rhs_flat = rhs_local.reshape(X * Y, Z)
    rhs_faces = jnp.concatenate([rhs_flat[:Y], rhs_flat[-Y:]], axis=0)
    faces = rhs_faces - operator_faces(solution, metric, helm, tables[:3], tables[3])
    return assemble(full, NP, faces=(faces[:Y], faces[Y:]))


def chebyshev(solution, rhs_local, metric, helm, tables, inverse, first_residual):
    centre = (upper_bound + lower_bound) / 2.0
    half_width = (upper_bound - lower_bound) / 2.0
    aspect = centre / half_width
    weight_prev = 1.0 / aspect
    if first_residual is not None:
        residual = first_residual
    else:
        residual = residual_of(solution, rhs_local, metric, helm, tables)
    update = inverse * residual / centre
    solution = solution + update
    residual = residual_of(solution, rhs_local, metric, helm, tables)
    weight_next = 1.0 / (2.0 * aspect - weight_prev)
    update = (
        weight_next * weight_prev * update + 2.0 * weight_next / half_width * inverse * residual
    )
    solution = solution + update
    return solution


def local(rhs_local, metric, helm, columns, live_blocks, block_values):
    derivative, linear = gll_tables(NP)
    shape = rhs_local.shape
    nw = lax.axis_size("wide")
    copies = (shape[0] // NP, shape[1] // NP, block_extent() // NP)
    tables = big_tables(derivative, shape)
    face_y = jnp.asarray(np.kron(np.eye(2 * shape[1] // NP, dtype=np.float32), derivative))
    tables = tables + (face_y,)
    sx, sy, sz = big_tables(derivative * derivative, shape)
    down_tables = tuple((repeat_table(linear.T, copies[axis]) for axis in range(3)))
    up_tables = tuple((repeat_table(linear, copies[axis]) for axis in range(3)))

    rows = shape[0] * shape[1]
    diagonal = (
        helm.reshape(rows, -1)
        + jnp.dot(sx.T, metric[0].reshape(rows, -1), precision=fast)
        + jnp.dot(sy.T, metric[1].reshape(rows, -1), precision=fast)
        + jnp.dot(metric[2].reshape(rows, -1), sz, precision=fast)
    ).reshape(shape)
    mats = jnp.concatenate(
        [
            block_values[0, 0].reshape(-1),
            columns[0, 0].astype(jnp.float32).reshape(-1),
            live_blocks[0, 0].astype(jnp.float32),
        ]
    )
    both, mats = assemble(jnp.stack([diagonal, rhs_local]), NP, mats)
    nvals = block_values.shape[2] * block_values.shape[3]
    ncols = columns.shape[2] * columns.shape[3]
    next_values = mats[:nvals].reshape(block_values.shape[2:])
    next_columns = mats[nvals : nvals + ncols].astype(jnp.int32).reshape(columns.shape[2:])
    next_live = mats[nvals + ncols :].astype(jnp.int32)
    inverse = 1.0 / both[0]
    first = chebyshev(
        jnp.zeros_like(rhs_local), rhs_local, metric, helm, tables, inverse, both[1]
    )
    local_res = rhs_local - apply_operator(first, metric, helm, tables)
    corners = local_res
    for axis in range(3):
        corners = contract(corners, down_tables[axis], axis)

    cx, cy, cz = corners.shape
    ext = jnp.concatenate([shift(corners, 0, -1), corners, shift(corners, 0, 1)], axis=1)
    qz = ext[:, :, 0::2] + jnp.roll(ext, 1, axis=2)[:, :, 0::2]
    qy = qz[:, cy : cy + 7 : 2] + qz[:, cy - 1 : cy + 6 : 2]
    zero = jnp.zeros_like(qy[:1])
    qx = jnp.concatenate([zero, qy, zero], axis=0)
    partial = qx[1 : cx + 2 : 2] + qx[0 : cx + 1 : 2]

    sent = jnp.stack(
        [jnp.roll(partial, 1, axis=2), partial, jnp.roll(partial, -1, axis=2)], axis=-1
    )
    sent = jnp.transpose(sent, (2, 0, 1, 3))
    got = lax.all_to_all(sent, "wide", 0, 0, tiled=True)
    even = got[:, 0] + jnp.roll(got[:, 2], 1, axis=0)
    got = jnp.stack([even, got[:, 1]], axis=1)
    frame = jnp.transpose(got, (3, 2, 0, 1)).reshape(3, 4, -1)
    span = frame.shape[2]
    nxb = span // BS
    frame_rows = frame.reshape(-1, BS)

    cols = jnp.concatenate([columns[0], next_columns[None]], axis=0)
    lives = jnp.concatenate([live_blocks[0], next_live[None]], axis=0)
    vals = jnp.concatenate([block_values[0], next_values[None]], axis=0)
    y_off = jnp.array([0, 0, 2], jnp.int32)[:, None, None]
    layer = cols // (2 * nxb)
    block = cols % (2 * nxb)
    index = (layer * 4 + y_off + block // nxb) * nxb + block % nxb
    picked = jnp.take(frame_rows, index.reshape(-1), axis=0).reshape(index.shape + (BS,))
    live = (jnp.arange(K, dtype=jnp.int32)[None, None, :] < lives[:, :, None]).astype(
        jnp.float32
    )
    values = vals.reshape(vals.shape[:2] + (K, BS, BS))
    product = jnp.einsum("yxkij,yxkj,yxk->yxi", values, picked, live, precision=highest)
    product = product.reshape(3, span)
    coarse_product = product[:2].reshape(1, 2, span)

    pick = (2 * np.arange(nw)[:, None] + np.arange(3)[None, :]) % span
    back = jnp.transpose(product[:, pick], (1, 0, 2))
    got = lax.all_to_all(back, "wide", 0, 0, tiled=True)
    hx = jnp.stack([got[:, :, 0:2], got[:, :, 1:3]], axis=-1).reshape(nw, 3, 4)
    hy = jnp.stack([hx[:, 0:2], hx[:, 1:3]], axis=2).reshape(nw, 4, 4)
    hz = jnp.stack([hy, jnp.roll(hy, -1, axis=0)], axis=1).reshape(2 * nw, 4, 4)
    correction = jnp.transpose(hz, (2, 1, 0))
    for axis in range(3):
        correction = contract(correction, up_tables[axis], axis)
    second = first + correction
    smoothed = chebyshev(second, rhs_local, metric, helm, tables, inverse, None)
    return (smoothed, coarse_product)


def solution(mesh):
    placed = (
        P("wide", "deep", None),
        P(None, "wide", "deep", None),
        P("wide", "deep", None),
        P("wide", "deep", None, None),
        P("wide", "deep", None),
        P("wide", "deep", None, None),
    )
    return jax.shard_map(
        local,
        mesh=mesh,
        in_specs=placed,
        out_specs=(P("wide", "deep", None), P("wide", "deep", None)),
        check_vma=False,
    )
```

```python
import jax
import jax.numpy as jnp
import numpy as np
from jax import lax
from jax.sharding import PartitionSpec as P

NP = 8
K = 8
BS = 8


upper_bound = 6.0
lower_bound = 0.6
highest = lax.Precision.HIGHEST
fast = lax.Precision.HIGH


def gll_tables(count):
    order = count - 1
    nodes = np.cos(np.pi * np.arange(count) / order)
    legendre = np.zeros((count, count))
    for sweep in range(101):
        legendre[:, 0] = 1.0
        legendre[:, 1] = nodes
        for degree in range(2, count):
            legendre[:, degree] = (
                (2 * degree - 1) * nodes * legendre[:, degree - 1]
                - (degree - 1) * legendre[:, degree - 2]
            ) / degree
        if sweep < 100:
            nodes = nodes - (nodes * legendre[:, order] - legendre[:, order - 1]) / (
                count * legendre[:, order]
            )
    nodes = nodes[::-1].copy()
    values = legendre[::-1, order].copy()
    identity_table = np.eye(count)
    spacing = nodes[:, None] - nodes[None, :] + identity_table
    derivative = values[:, None] / values[None, :] / spacing
    derivative = derivative * (1.0 - identity_table)
    derivative[0, 0] = -order * (order + 1) / 4.0
    derivative[-1, -1] = order * (order + 1) / 4.0
    linear = np.stack([(1.0 - nodes) / 2.0, (1.0 + nodes) / 2.0], axis=1)
    return (np.asarray(derivative, np.float32), np.asarray(linear, np.float32))


def block_extent():
    return 128


def repeat_table(small, copies):
    return jnp.asarray(np.kron(np.eye(copies, dtype=np.float32), small))


def contract(field, table, axis):
    if axis == 0:
        return jnp.einsum("mi,iyz->myz", table, field, precision=highest)
    if axis == 1:
        return jnp.einsum("mj,xjz->xmz", table, field, precision=highest)
    shape = field.shape
    blocked = table.shape[1]
    grid = field.reshape(shape[0], shape[1], shape[2] // blocked, blocked)
    result = jnp.einsum("mk,xynk->xynm", table, grid, precision=highest)
    return result.reshape(shape[0], shape[1], -1)


def shift(value, dw, dd):
    nw = lax.axis_size("wide")
    nd = lax.axis_size("deep")
    if dd == 0:
        pairs = [((w + dw) % nw, w) for w in range(nw)]
        return lax.ppermute(value, "wide", pairs)
    if dw == 0:
        pairs = [((d + dd) % nd, d) for d in range(nd)]
        return lax.ppermute(value, "deep", pairs)
    pairs = []
    for w in range(nw):
        for d in range(nd):
            src = ((w + dw) % nw) * nd + (d + dd) % nd
            pairs.append((src, w * nd + d))
    return lax.ppermute(value, ("wide", "deep"), pairs)


def node_mask(length, count, node, axis, ndim):
    index = lax.broadcasted_iota(jnp.int32, (length,), 0) % count == node
    shape = [1] * ndim
    shape[axis] = length
    return index.reshape(shape)


def assemble(field, count, carry=None):
    nd = field.ndim
    X, Y, Z = field.shape[-3:]
    lx = shift(field[..., -1, :, :], -1, 0)
    rx = shift(field[..., 0, :, :], 1, 0)
    ext = jnp.concatenate([lx[..., None, :, :], field, rx[..., None, :, :]], axis=-3)
    hi = node_mask(X, count, count - 1, nd - 3, nd)
    lo = node_mask(X, count, 0, nd - 3, nd)
    field = (
        ext[..., 1 : X + 1, :, :]
        + jnp.where(hi, ext[..., 2 : X + 2, :, :], 0.0)
        + jnp.where(lo, ext[..., 0:X, :, :], 0.0)
    )
    ly = shift(field[..., :, -1, :], 0, -1)
    face = field[..., :, 0, :]
    carried = None
    if carry is None:
        ry = shift(face, 0, 1)
    else:
        packed = shift(jnp.concatenate([face.reshape(-1), carry]), 0, 1)
        ry = packed[: face.size].reshape(face.shape)
        carried = packed[face.size :]
    ext = jnp.concatenate([ly[..., :, None, :], field, ry[..., :, None, :]], axis=-2)
    hi = node_mask(Y, count, count - 1, nd - 2, nd)
    lo = node_mask(Y, count, 0, nd - 2, nd)
    field = (
        ext[..., :, 1 : Y + 1, :]
        + jnp.where(hi, ext[..., :, 2 : Y + 2, :], 0.0)
        + jnp.where(lo, ext[..., :, 0:Y, :], 0.0)
    )
    hi = node_mask(Z, count, count - 1, nd - 1, nd)
    lo = node_mask(Z, count, 0, nd - 1, nd)
    field = (
        field
        + jnp.where(hi, jnp.roll(field, -1, axis=-1), 0.0)
        + jnp.where(lo, jnp.roll(field, 1, axis=-1), 0.0)
    )
    if carry is None:
        return field
    return field, carried


def apply_operator(field, metric, helm, tables):
    shape = field.shape
    flat = field.reshape(-1, shape[-1])
    total = helm.reshape(flat.shape) * flat
    tx, ty, tz = tables
    for axis, table in ((0, tx), (1, ty)):
        slope = jnp.dot(table, flat, precision=fast)
        weighted = metric[axis].reshape(flat.shape) * slope
        total = total + jnp.dot(table.T, weighted, precision=fast)
    slope = jnp.dot(flat, tz.T, precision=fast)
    weighted = metric[2].reshape(flat.shape) * slope
    total = total + jnp.dot(weighted, tz, precision=fast)
    return total.reshape(shape)


def big_tables(small, shape):
    X, Y, Z = shape
    n = small.shape[0]
    px = np.kron(np.kron(np.eye(X // n, dtype=np.float32), small), np.eye(Y, dtype=np.float32))
    py = np.kron(np.eye(X, dtype=np.float32), np.kron(np.eye(Y // n, dtype=np.float32), small))
    pz = np.kron(np.eye(Z // n, dtype=np.float32), small)
    return tuple(jnp.asarray(t) for t in (px, py, pz))


def chebyshev(solution, rhs_local, metric, helm, tables, inverse, first_residual):
    centre = (upper_bound + lower_bound) / 2.0
    half_width = (upper_bound - lower_bound) / 2.0
    aspect = centre / half_width
    weight_prev = 1.0 / aspect
    if first_residual is not None:
        residual = first_residual
    else:
        residual = assemble(rhs_local - apply_operator(solution, metric, helm, tables), NP)
    update = inverse * residual / centre
    solution = solution + update
    residual = assemble(rhs_local - apply_operator(solution, metric, helm, tables), NP)
    weight_next = 1.0 / (2.0 * aspect - weight_prev)
    update = (
        weight_next * weight_prev * update + 2.0 * weight_next / half_width * inverse * residual
    )
    solution = solution + update
    return solution


def local(rhs_local, metric, helm, columns, live_blocks, block_values):
    derivative, linear = gll_tables(NP)
    shape = rhs_local.shape
    nw = lax.axis_size("wide")
    copies = (shape[0] // NP, shape[1] // NP, block_extent() // NP)
    tables = big_tables(derivative, shape)
    sx, sy, sz = big_tables(derivative * derivative, shape)
    down_tables = tuple((repeat_table(linear.T, copies[axis]) for axis in range(3)))
    up_tables = tuple((repeat_table(linear, copies[axis]) for axis in range(3)))

    rows = shape[0] * shape[1]
    diagonal = (
        helm.reshape(rows, -1)
        + jnp.dot(sx.T, metric[0].reshape(rows, -1), precision=fast)
        + jnp.dot(sy.T, metric[1].reshape(rows, -1), precision=fast)
        + jnp.dot(metric[2].reshape(rows, -1), sz, precision=fast)
    ).reshape(shape)
    mats = jnp.concatenate(
        [
            block_values[0, 0].reshape(-1),
            columns[0, 0].astype(jnp.float32).reshape(-1),
            live_blocks[0, 0].astype(jnp.float32),
        ]
    )
    both, mats = assemble(jnp.stack([diagonal, rhs_local]), NP, mats)
    nvals = block_values.shape[2] * block_values.shape[3]
    ncols = columns.shape[2] * columns.shape[3]
    next_values = mats[:nvals].reshape(block_values.shape[2:])
    next_columns = mats[nvals : nvals + ncols].astype(jnp.int32).reshape(columns.shape[2:])
    next_live = mats[nvals + ncols :].astype(jnp.int32)
    inverse = 1.0 / both[0]
    first = chebyshev(
        jnp.zeros_like(rhs_local), rhs_local, metric, helm, tables, inverse, both[1]
    )
    local_res = rhs_local - apply_operator(first, metric, helm, tables)
    corners = local_res
    for axis in range(3):
        corners = contract(corners, down_tables[axis], axis)

    cx, cy, cz = corners.shape
    ext = jnp.concatenate([shift(corners, 0, -1), corners, shift(corners, 0, 1)], axis=1)
    qz = ext[:, :, 0::2] + jnp.roll(ext, 1, axis=2)[:, :, 0::2]
    qy = qz[:, cy : cy + 7 : 2] + qz[:, cy - 1 : cy + 6 : 2]
    zero = jnp.zeros_like(qy[:1])
    qx = jnp.concatenate([zero, qy, zero], axis=0)
    partial = qx[1 : cx + 2 : 2] + qx[0 : cx + 1 : 2]

    sent = jnp.stack(
        [jnp.roll(partial, 1, axis=2), partial, jnp.roll(partial, -1, axis=2)], axis=-1
    )
    sent = jnp.transpose(sent, (2, 0, 1, 3))
    got = lax.all_to_all(sent, "wide", 0, 0, tiled=True)
    even = got[:, 0] + jnp.roll(got[:, 2], 1, axis=0)
    got = jnp.stack([even, got[:, 1]], axis=1)
    frame = jnp.transpose(got, (3, 2, 0, 1)).reshape(3, 4, -1)
    span = frame.shape[2]
    nxb = span // BS
    frame_rows = frame.reshape(-1, BS)

    cols = jnp.concatenate([columns[0], next_columns[None]], axis=0)
    lives = jnp.concatenate([live_blocks[0], next_live[None]], axis=0)
    vals = jnp.concatenate([block_values[0], next_values[None]], axis=0)
    y_off = jnp.array([0, 0, 2], jnp.int32)[:, None, None]
    layer = cols // (2 * nxb)
    block = cols % (2 * nxb)
    index = (layer * 4 + y_off + block // nxb) * nxb + block % nxb
    picked = jnp.take(frame_rows, index.reshape(-1), axis=0, mode="clip").reshape(index.shape + (BS,))
    live = (jnp.arange(K, dtype=jnp.int32)[None, None, :] < lives[:, :, None]).astype(
        jnp.float32
    )
    values = vals.reshape(vals.shape[:2] + (K, BS, BS)) * live[..., None, None]
    values = lax.optimization_barrier(values)
    product = jnp.einsum("yxkij,yxkj->yxi", values, picked, precision=highest)
    product = product.reshape(3, span)
    coarse_product = product[:2].reshape(1, 2, span)

    back = jnp.stack(
        [product[:, 0::2], product[:, 1::2], jnp.roll(product, -2, axis=1)[:, 0::2]], axis=-1
    )
    back = jnp.transpose(back, (1, 0, 2))
    got = lax.all_to_all(back, "wide", 0, 0, tiled=True)
    hx = jnp.stack([got[:, :, 0:2], got[:, :, 1:3]], axis=-1).reshape(nw, 3, 4)
    hy = jnp.stack([hx[:, 0:2], hx[:, 1:3]], axis=2).reshape(nw, 4, 4)
    hz = jnp.stack([hy, jnp.roll(hy, -1, axis=0)], axis=1).reshape(2 * nw, 4, 4)
    correction = jnp.transpose(hz, (2, 1, 0))
    for axis in range(3):
        correction = contract(correction, up_tables[axis], axis)
    second = first + correction
    smoothed = chebyshev(second, rhs_local, metric, helm, tables, inverse, None)
    return (smoothed, coarse_product)


def solution(mesh):
    placed = (
        P("wide", "deep", None),
        P(None, "wide", "deep", None),
        P("wide", "deep", None),
        P("wide", "deep", None, None),
        P("wide", "deep", None),
        P("wide", "deep", None, None),
    )
    return jax.shard_map(
        local,
        mesh=mesh,
        in_specs=placed,
        out_specs=(P("wide", "deep", None), P("wide", "deep", None)),
        check_vma=False,
    )
```

```python
import jax
import jax.numpy as jnp
import numpy as np
from jax import lax
from jax.sharding import PartitionSpec as P

NP = 8
K = 8
BS = 8


upper_bound = 6.0
lower_bound = 0.6
highest = lax.Precision.HIGHEST
fast = lax.Precision.HIGH


def gll_tables(count):
    order = count - 1
    nodes = np.cos(np.pi * np.arange(count) / order)
    legendre = np.zeros((count, count))
    for sweep in range(101):
        legendre[:, 0] = 1.0
        legendre[:, 1] = nodes
        for degree in range(2, count):
            legendre[:, degree] = (
                (2 * degree - 1) * nodes * legendre[:, degree - 1]
                - (degree - 1) * legendre[:, degree - 2]
            ) / degree
        if sweep < 100:
            nodes = nodes - (nodes * legendre[:, order] - legendre[:, order - 1]) / (
                count * legendre[:, order]
            )
    nodes = nodes[::-1].copy()
    values = legendre[::-1, order].copy()
    identity_table = np.eye(count)
    spacing = nodes[:, None] - nodes[None, :] + identity_table
    derivative = values[:, None] / values[None, :] / spacing
    derivative = derivative * (1.0 - identity_table)
    derivative[0, 0] = -order * (order + 1) / 4.0
    derivative[-1, -1] = order * (order + 1) / 4.0
    linear = np.stack([(1.0 - nodes) / 2.0, (1.0 + nodes) / 2.0], axis=1)
    return (np.asarray(derivative, np.float32), np.asarray(linear, np.float32))


def block_extent():
    return 128


def repeat_table(small, copies):
    return jnp.asarray(np.kron(np.eye(copies, dtype=np.float32), small))


def contract(field, table, axis):
    if axis == 0:
        return jnp.einsum("mi,iyz->myz", table, field, precision=highest)
    if axis == 1:
        return jnp.einsum("mj,xjz->xmz", table, field, precision=highest)
    shape = field.shape
    blocked = table.shape[1]
    grid = field.reshape(shape[0], shape[1], shape[2] // blocked, blocked)
    result = jnp.einsum("mk,xynk->xynm", table, grid, precision=highest)
    return result.reshape(shape[0], shape[1], -1)


def shift(value, dw, dd):
    nw = lax.axis_size("wide")
    nd = lax.axis_size("deep")
    if dd == 0:
        pairs = [((w + dw) % nw, w) for w in range(nw)]
        return lax.ppermute(value, "wide", pairs)
    if dw == 0:
        pairs = [((d + dd) % nd, d) for d in range(nd)]
        return lax.ppermute(value, "deep", pairs)
    pairs = []
    for w in range(nw):
        for d in range(nd):
            src = ((w + dw) % nw) * nd + (d + dd) % nd
            pairs.append((src, w * nd + d))
    return lax.ppermute(value, ("wide", "deep"), pairs)


def node_mask(length, count, node, axis, ndim):
    index = lax.broadcasted_iota(jnp.int32, (length,), 0) % count == node
    shape = [1] * ndim
    shape[axis] = length
    return index.reshape(shape)


def assemble(field, count, carry=None):
    nd = field.ndim
    X, Y, Z = field.shape[-3:]
    lx = shift(field[..., -1, :, :], -1, 0)
    rx = shift(field[..., 0, :, :], 1, 0)
    ext = jnp.concatenate([lx[..., None, :, :], field, rx[..., None, :, :]], axis=-3)
    hi = node_mask(X, count, count - 1, nd - 3, nd)
    lo = node_mask(X, count, 0, nd - 3, nd)
    field = (
        ext[..., 1 : X + 1, :, :]
        + jnp.where(hi, ext[..., 2 : X + 2, :, :], 0.0)
        + jnp.where(lo, ext[..., 0:X, :, :], 0.0)
    )
    ly = shift(field[..., :, -1, :], 0, -1)
    face = field[..., :, 0, :]
    carried = None
    if carry is None:
        ry = shift(face, 0, 1)
    else:
        packed = shift(jnp.concatenate([face.reshape(-1), carry]), 0, 1)
        ry = packed[: face.size].reshape(face.shape)
        carried = packed[face.size :]
    ext = jnp.concatenate([ly[..., :, None, :], field, ry[..., :, None, :]], axis=-2)
    hi = node_mask(Y, count, count - 1, nd - 2, nd)
    lo = node_mask(Y, count, 0, nd - 2, nd)
    field = (
        ext[..., :, 1 : Y + 1, :]
        + jnp.where(hi, ext[..., :, 2 : Y + 2, :], 0.0)
        + jnp.where(lo, ext[..., :, 0:Y, :], 0.0)
    )
    hi = node_mask(Z, count, count - 1, nd - 1, nd)
    lo = node_mask(Z, count, 0, nd - 1, nd)
    field = (
        field
        + jnp.where(hi, jnp.roll(field, -1, axis=-1), 0.0)
        + jnp.where(lo, jnp.roll(field, 1, axis=-1), 0.0)
    )
    if carry is None:
        return field
    return field, carried


def apply_operator(field, metric, helm, tables):
    shape = field.shape
    flat = field.reshape(-1, shape[-1])
    total = helm.reshape(flat.shape) * flat
    tx, ty, tz = tables
    for axis, table in ((0, tx), (1, ty)):
        slope = jnp.dot(table, flat, precision=fast)
        weighted = metric[axis].reshape(flat.shape) * slope
        total = total + jnp.dot(table.T, weighted, precision=fast)
    slope = jnp.dot(flat, tz.T, precision=fast)
    weighted = metric[2].reshape(flat.shape) * slope
    total = total + jnp.dot(weighted, tz, precision=fast)
    return total.reshape(shape)


def big_tables(small, shape):
    X, Y, Z = shape
    n = small.shape[0]
    px = np.kron(np.kron(np.eye(X // n, dtype=np.float32), small), np.eye(Y, dtype=np.float32))
    py = np.kron(np.eye(X, dtype=np.float32), np.kron(np.eye(Y // n, dtype=np.float32), small))
    pz = np.kron(np.eye(Z // n, dtype=np.float32), small)
    return tuple(jnp.asarray(t) for t in (px, py, pz))


def chebyshev(solution, rhs_local, metric, helm, tables, inverse, first_residual):
    centre = (upper_bound + lower_bound) / 2.0
    half_width = (upper_bound - lower_bound) / 2.0
    aspect = centre / half_width
    weight_prev = 1.0 / aspect
    if first_residual is not None:
        residual = first_residual
    else:
        residual = assemble(rhs_local - apply_operator(solution, metric, helm, tables), NP)
    update = inverse * residual / centre
    solution = solution + update
    residual = assemble(rhs_local - apply_operator(solution, metric, helm, tables), NP)
    weight_next = 1.0 / (2.0 * aspect - weight_prev)
    update = (
        weight_next * weight_prev * update + 2.0 * weight_next / half_width * inverse * residual
    )
    solution = solution + update
    return solution


def local(rhs_local, metric, helm, columns, live_blocks, block_values):
    derivative, linear = gll_tables(NP)
    shape = rhs_local.shape
    nw = lax.axis_size("wide")
    copies = (shape[0] // NP, shape[1] // NP, block_extent() // NP)
    tables = big_tables(derivative, shape)
    sx, sy, sz = big_tables(derivative * derivative, shape)
    down_tables = tuple((repeat_table(linear.T, copies[axis]) for axis in range(3)))
    up_tables = tuple((repeat_table(linear, copies[axis]) for axis in range(3)))

    rows = shape[0] * shape[1]
    diagonal = (
        helm.reshape(rows, -1)
        + jnp.dot(sx.T, metric[0].reshape(rows, -1), precision=fast)
        + jnp.dot(sy.T, metric[1].reshape(rows, -1), precision=fast)
        + jnp.dot(metric[2].reshape(rows, -1), sz, precision=fast)
    ).reshape(shape)
    mats = jnp.concatenate(
        [
            block_values[0, 0].reshape(-1),
            columns[0, 0].astype(jnp.float32).reshape(-1),
            live_blocks[0, 0].astype(jnp.float32),
        ]
    )
    both, mats = assemble(jnp.stack([diagonal, rhs_local]), NP, mats)
    nvals = block_values.shape[2] * block_values.shape[3]
    ncols = columns.shape[2] * columns.shape[3]
    next_values = mats[:nvals].reshape(block_values.shape[2:])
    next_columns = mats[nvals : nvals + ncols].astype(jnp.int32).reshape(columns.shape[2:])
    next_live = mats[nvals + ncols :].astype(jnp.int32)
    inverse = 1.0 / both[0]
    first = chebyshev(
        jnp.zeros_like(rhs_local), rhs_local, metric, helm, tables, inverse, both[1]
    )
    local_res = rhs_local - apply_operator(first, metric, helm, tables)
    corners = local_res
    for axis in range(3):
        corners = contract(corners, down_tables[axis], axis)

    cx, cy, cz = corners.shape
    ext = jnp.concatenate([shift(corners, 0, -1), corners, shift(corners, 0, 1)], axis=1)
    qz = ext[:, :, 0::2] + jnp.roll(ext, 1, axis=2)[:, :, 0::2]
    qy = qz[:, cy : cy + 7 : 2] + qz[:, cy - 1 : cy + 6 : 2]
    zero = jnp.zeros_like(qy[:1])
    qx = jnp.concatenate([zero, qy, zero], axis=0)
    partial = qx[1 : cx + 2 : 2] + qx[0 : cx + 1 : 2]

    sent = jnp.stack(
        [jnp.roll(partial, 1, axis=2), partial, jnp.roll(partial, -1, axis=2)], axis=-1
    )
    sent = jnp.transpose(sent, (2, 0, 1, 3))
    got = lax.all_to_all(sent, "wide", 0, 0, tiled=True)
    even = got[:, 0] + jnp.roll(got[:, 2], 1, axis=0)
    got = jnp.stack([even, got[:, 1]], axis=1)
    frame = jnp.transpose(got, (3, 2, 0, 1)).reshape(3, 4, -1)
    span = frame.shape[2]
    nxb = span // BS
    frame_rows = frame.reshape(-1, BS)

    cols = jnp.concatenate([columns[0], next_columns[None]], axis=0)
    lives = jnp.concatenate([live_blocks[0], next_live[None]], axis=0)
    vals = jnp.concatenate([block_values[0], next_values[None]], axis=0)
    y_off = jnp.array([0, 0, 2], jnp.int32)[:, None, None]
    layer = cols // (2 * nxb)
    block = cols % (2 * nxb)
    index = (layer * 4 + y_off + block // nxb) * nxb + block % nxb
    picked = jnp.take(frame_rows, index.reshape(-1), axis=0, mode="clip").reshape(index.shape + (BS,))
    live = (jnp.arange(K, dtype=jnp.int32)[None, None, :] < lives[:, :, None]).astype(
        jnp.float32
    )
    values = vals.reshape(vals.shape[:2] + (K, BS, BS))
    product = jnp.einsum("yxkij,yxkj,yxk->yxi", values, picked, live, precision=highest)
    product = product.reshape(3, span)
    coarse_product = product[:2].reshape(1, 2, span)

    pick = (2 * np.arange(nw)[:, None] + np.arange(3)[None, :]) % span
    back = jnp.transpose(product[:, pick], (1, 0, 2))
    got = lax.all_to_all(back, "wide", 0, 0, tiled=True)
    hx = jnp.stack([got[:, :, 0:2], got[:, :, 1:3]], axis=-1).reshape(nw, 3, 4)
    hy = jnp.stack([hx[:, 0:2], hx[:, 1:3]], axis=2).reshape(nw, 4, 4)
    hz = jnp.stack([hy, jnp.roll(hy, -1, axis=0)], axis=1).reshape(2 * nw, 4, 4)
    correction = jnp.transpose(hz, (2, 1, 0))
    for axis in range(3):
        correction = contract(correction, up_tables[axis], axis)
    second = first + correction
    smoothed = chebyshev(second, rhs_local, metric, helm, tables, inverse, None)
    return (smoothed, coarse_product)


def solution(mesh):
    placed = (
        P("wide", "deep", None),
        P(None, "wide", "deep", None),
        P("wide", "deep", None),
        P("wide", "deep", None, None),
        P("wide", "deep", None),
        P("wide", "deep", None, None),
    )
    return jax.shard_map(
        local,
        mesh=mesh,
        in_specs=placed,
        out_specs=(P("wide", "deep", None), P("wide", "deep", None)),
        check_vma=False,
    )
```

```python
import jax
import jax.numpy as jnp
import numpy as np
from jax import lax
from jax.sharding import PartitionSpec as P

NP = 8
K = 8
BS = 8


upper_bound = 6.0
lower_bound = 0.6
highest = lax.Precision.HIGHEST
fast = lax.Precision.HIGH


def gll_tables(count):
    order = count - 1
    nodes = np.cos(np.pi * np.arange(count) / order)
    legendre = np.zeros((count, count))
    for sweep in range(101):
        legendre[:, 0] = 1.0
        legendre[:, 1] = nodes
        for degree in range(2, count):
            legendre[:, degree] = (
                (2 * degree - 1) * nodes * legendre[:, degree - 1]
                - (degree - 1) * legendre[:, degree - 2]
            ) / degree
        if sweep < 100:
            nodes = nodes - (nodes * legendre[:, order] - legendre[:, order - 1]) / (
                count * legendre[:, order]
            )
    nodes = nodes[::-1].copy()
    values = legendre[::-1, order].copy()
    identity_table = np.eye(count)
    spacing = nodes[:, None] - nodes[None, :] + identity_table
    derivative = values[:, None] / values[None, :] / spacing
    derivative = derivative * (1.0 - identity_table)
    derivative[0, 0] = -order * (order + 1) / 4.0
    derivative[-1, -1] = order * (order + 1) / 4.0
    linear = np.stack([(1.0 - nodes) / 2.0, (1.0 + nodes) / 2.0], axis=1)
    return (np.asarray(derivative, np.float32), np.asarray(linear, np.float32))


def block_extent():
    return 128


def repeat_table(small, copies):
    return jnp.asarray(np.kron(np.eye(copies, dtype=np.float32), small))


def contract(field, table, axis):
    if axis == 0:
        return jnp.einsum("mi,iyz->myz", table, field, precision=fast)
    if axis == 1:
        return jnp.einsum("mj,xjz->xmz", table, field, precision=fast)
    shape = field.shape
    blocked = table.shape[1]
    grid = field.reshape(shape[0], shape[1], shape[2] // blocked, blocked)
    result = jnp.einsum("mk,xynk->xynm", table, grid, precision=fast)
    return result.reshape(shape[0], shape[1], -1)


def shift(value, dw, dd):
    nw = lax.axis_size("wide")
    nd = lax.axis_size("deep")
    if dd == 0:
        pairs = [((w + dw) % nw, w) for w in range(nw)]
        return lax.ppermute(value, "wide", pairs)
    if dw == 0:
        pairs = [((d + dd) % nd, d) for d in range(nd)]
        return lax.ppermute(value, "deep", pairs)
    pairs = []
    for w in range(nw):
        for d in range(nd):
            src = ((w + dw) % nw) * nd + (d + dd) % nd
            pairs.append((src, w * nd + d))
    return lax.ppermute(value, ("wide", "deep"), pairs)


def node_mask(length, count, node, axis, ndim):
    index = lax.broadcasted_iota(jnp.int32, (length,), 0) % count == node
    shape = [1] * ndim
    shape[axis] = length
    return index.reshape(shape)


def assemble(field, count, carry=None):
    nd = field.ndim
    X, Y, Z = field.shape[-3:]
    lx = shift(field[..., -1, :, :], -1, 0)
    rx = shift(field[..., 0, :, :], 1, 0)
    ext = jnp.concatenate([lx[..., None, :, :], field, rx[..., None, :, :]], axis=-3)
    hi = node_mask(X, count, count - 1, nd - 3, nd)
    lo = node_mask(X, count, 0, nd - 3, nd)
    field = (
        ext[..., 1 : X + 1, :, :]
        + jnp.where(hi, ext[..., 2 : X + 2, :, :], 0.0)
        + jnp.where(lo, ext[..., 0:X, :, :], 0.0)
    )
    ly = shift(field[..., :, -1, :], 0, -1)
    face = field[..., :, 0, :]
    carried = None
    if carry is None:
        ry = shift(face, 0, 1)
    else:
        packed = shift(jnp.concatenate([face.reshape(-1), carry]), 0, 1)
        ry = packed[: face.size].reshape(face.shape)
        carried = packed[face.size :]
    ext = jnp.concatenate([ly[..., :, None, :], field, ry[..., :, None, :]], axis=-2)
    hi = node_mask(Y, count, count - 1, nd - 2, nd)
    lo = node_mask(Y, count, 0, nd - 2, nd)
    field = (
        ext[..., :, 1 : Y + 1, :]
        + jnp.where(hi, ext[..., :, 2 : Y + 2, :], 0.0)
        + jnp.where(lo, ext[..., :, 0:Y, :], 0.0)
    )
    hi = node_mask(Z, count, count - 1, nd - 1, nd)
    lo = node_mask(Z, count, 0, nd - 1, nd)
    field = (
        field
        + jnp.where(hi, jnp.roll(field, -1, axis=-1), 0.0)
        + jnp.where(lo, jnp.roll(field, 1, axis=-1), 0.0)
    )
    if carry is None:
        return field
    return field, carried


def apply_operator(field, metric, helm, tables):
    shape = field.shape
    flat = field.reshape(-1, shape[-1])
    total = helm.reshape(flat.shape) * flat
    tx, ty, tz = tables
    for axis, table in ((0, tx), (1, ty)):
        slope = jnp.dot(table, flat, precision=fast)
        weighted = metric[axis].reshape(flat.shape) * slope
        total = total + jnp.dot(table.T, weighted, precision=fast)
    slope = jnp.dot(flat, tz.T, precision=fast)
    weighted = metric[2].reshape(flat.shape) * slope
    total = total + jnp.dot(weighted, tz, precision=fast)
    return total.reshape(shape)


def big_tables(small, shape):
    X, Y, Z = shape
    n = small.shape[0]
    px = np.kron(np.kron(np.eye(X // n, dtype=np.float32), small), np.eye(Y, dtype=np.float32))
    py = np.kron(np.eye(X, dtype=np.float32), np.kron(np.eye(Y // n, dtype=np.float32), small))
    pz = np.kron(np.eye(Z // n, dtype=np.float32), small)
    return tuple(jnp.asarray(t) for t in (px, py, pz))


def chebyshev(solution, rhs_local, metric, helm, tables, inverse, first_residual):
    centre = (upper_bound + lower_bound) / 2.0
    half_width = (upper_bound - lower_bound) / 2.0
    aspect = centre / half_width
    weight_prev = 1.0 / aspect
    if first_residual is not None:
        residual = first_residual
    else:
        residual = assemble(rhs_local - apply_operator(solution, metric, helm, tables), NP)
    update = inverse * residual / centre
    solution = solution + update
    residual = assemble(rhs_local - apply_operator(solution, metric, helm, tables), NP)
    weight_next = 1.0 / (2.0 * aspect - weight_prev)
    update = (
        weight_next * weight_prev * update + 2.0 * weight_next / half_width * inverse * residual
    )
    solution = solution + update
    return solution


def local(rhs_local, metric, helm, columns, live_blocks, block_values):
    derivative, linear = gll_tables(NP)
    shape = rhs_local.shape
    nw = lax.axis_size("wide")
    copies = (shape[0] // NP, shape[1] // NP, block_extent() // NP)
    tables = big_tables(derivative, shape)
    sx, sy, sz = big_tables(derivative * derivative, shape)
    down_tables = tuple((repeat_table(linear.T, copies[axis]) for axis in range(3)))
    up_tables = tuple((repeat_table(linear, copies[axis]) for axis in range(3)))

    rows = shape[0] * shape[1]
    diagonal = (
        helm.reshape(rows, -1)
        + jnp.dot(sx.T, metric[0].reshape(rows, -1), precision=fast)
        + jnp.dot(sy.T, metric[1].reshape(rows, -1), precision=fast)
        + jnp.dot(metric[2].reshape(rows, -1), sz, precision=fast)
    ).reshape(shape)
    mats = jnp.concatenate(
        [
            block_values[0, 0].reshape(-1),
            columns[0, 0].astype(jnp.float32).reshape(-1),
            live_blocks[0, 0].astype(jnp.float32),
        ]
    )
    both, mats = assemble(jnp.stack([diagonal, rhs_local]), NP, mats)
    nvals = block_values.shape[2] * block_values.shape[3]
    ncols = columns.shape[2] * columns.shape[3]
    next_values = mats[:nvals].reshape(block_values.shape[2:])
    next_columns = mats[nvals : nvals + ncols].astype(jnp.int32).reshape(columns.shape[2:])
    next_live = mats[nvals + ncols :].astype(jnp.int32)
    inverse = 1.0 / both[0]
    first = chebyshev(
        jnp.zeros_like(rhs_local), rhs_local, metric, helm, tables, inverse, both[1]
    )
    local_res = rhs_local - apply_operator(first, metric, helm, tables)
    corners = local_res
    for axis in range(3):
        corners = contract(corners, down_tables[axis], axis)

    cx, cy, cz = corners.shape
    ext = jnp.concatenate([shift(corners, 0, -1), corners, shift(corners, 0, 1)], axis=1)
    qz = ext[:, :, 0::2] + jnp.roll(ext, 1, axis=2)[:, :, 0::2]
    qy = qz[:, cy : cy + 7 : 2] + qz[:, cy - 1 : cy + 6 : 2]
    zero = jnp.zeros_like(qy[:1])
    qx = jnp.concatenate([zero, qy, zero], axis=0)
    partial = qx[1 : cx + 2 : 2] + qx[0 : cx + 1 : 2]

    sent = jnp.stack(
        [jnp.roll(partial, 1, axis=2), partial, jnp.roll(partial, -1, axis=2)], axis=-1
    )
    sent = jnp.transpose(sent, (2, 0, 1, 3))
    got = lax.all_to_all(sent, "wide", 0, 0, tiled=True)
    even = got[:, 0] + jnp.roll(got[:, 2], 1, axis=0)
    got = jnp.stack([even, got[:, 1]], axis=1)
    frame = jnp.transpose(got, (3, 2, 0, 1)).reshape(3, 4, -1)
    span = frame.shape[2]
    nxb = span // BS
    frame_rows = frame.reshape(-1, BS)

    cols = jnp.concatenate([columns[0], next_columns[None]], axis=0)
    lives = jnp.concatenate([live_blocks[0], next_live[None]], axis=0)
    vals = jnp.concatenate([block_values[0], next_values[None]], axis=0)
    y_off = jnp.array([0, 0, 2], jnp.int32)[:, None, None]
    layer = cols // (2 * nxb)
    block = cols % (2 * nxb)
    index = (layer * 4 + y_off + block // nxb) * nxb + block % nxb
    picked = jnp.take(frame_rows, index.reshape(-1), axis=0).reshape(index.shape + (BS,))
    live = (jnp.arange(K, dtype=jnp.int32)[None, None, :] < lives[:, :, None]).astype(
        jnp.float32
    )
    values = vals.reshape(vals.shape[:2] + (K, BS, BS))
    product = jnp.einsum("yxkij,yxkj,yxk->yxi", values, picked, live, precision=highest)
    product = product.reshape(3, span)
    coarse_product = product[:2].reshape(1, 2, span)

    pick = (2 * np.arange(nw)[:, None] + np.arange(3)[None, :]) % span
    back = jnp.transpose(product[:, pick], (1, 0, 2))
    got = lax.all_to_all(back, "wide", 0, 0, tiled=True)
    hx = jnp.stack([got[:, :, 0:2], got[:, :, 1:3]], axis=-1).reshape(nw, 3, 4)
    hy = jnp.stack([hx[:, 0:2], hx[:, 1:3]], axis=2).reshape(nw, 4, 4)
    hz = jnp.stack([hy, jnp.roll(hy, -1, axis=0)], axis=1).reshape(2 * nw, 4, 4)
    correction = jnp.transpose(hz, (2, 1, 0))
    for axis in range(3):
        correction = contract(correction, up_tables[axis], axis)
    second = first + correction
    smoothed = chebyshev(second, rhs_local, metric, helm, tables, inverse, None)
    return (smoothed, coarse_product)


def solution(mesh):
    placed = (
        P("wide", "deep", None),
        P(None, "wide", "deep", None),
        P("wide", "deep", None),
        P("wide", "deep", None, None),
        P("wide", "deep", None),
        P("wide", "deep", None, None),
    )
    return jax.shard_map(
        local,
        mesh=mesh,
        in_specs=placed,
        out_specs=(P("wide", "deep", None), P("wide", "deep", None)),
        check_vma=False,
    )
```

```python
import jax
import jax.numpy as jnp
import numpy as np
from jax import lax
from jax.sharding import PartitionSpec as P

NP = 8
K = 8
BS = 8


upper_bound = 6.0
lower_bound = 0.6
highest = lax.Precision.HIGHEST
fast = lax.Precision.HIGH


def gll_tables(count):
    order = count - 1
    nodes = np.cos(np.pi * np.arange(count) / order)
    legendre = np.zeros((count, count))
    for sweep in range(101):
        legendre[:, 0] = 1.0
        legendre[:, 1] = nodes
        for degree in range(2, count):
            legendre[:, degree] = (
                (2 * degree - 1) * nodes * legendre[:, degree - 1]
                - (degree - 1) * legendre[:, degree - 2]
            ) / degree
        if sweep < 100:
            nodes = nodes - (nodes * legendre[:, order] - legendre[:, order - 1]) / (
                count * legendre[:, order]
            )
    nodes = nodes[::-1].copy()
    values = legendre[::-1, order].copy()
    identity_table = np.eye(count)
    spacing = nodes[:, None] - nodes[None, :] + identity_table
    derivative = values[:, None] / values[None, :] / spacing
    derivative = derivative * (1.0 - identity_table)
    derivative[0, 0] = -order * (order + 1) / 4.0
    derivative[-1, -1] = order * (order + 1) / 4.0
    linear = np.stack([(1.0 - nodes) / 2.0, (1.0 + nodes) / 2.0], axis=1)
    return (np.asarray(derivative, np.float32), np.asarray(linear, np.float32))


def block_extent():
    return 128


def repeat_table(small, copies):
    return jnp.asarray(np.kron(np.eye(copies, dtype=np.float32), small))


def contract(field, table, axis):
    if axis == 0:
        return jnp.einsum("mi,iyz->myz", table, field, precision=highest)
    if axis == 1:
        return jnp.einsum("mj,xjz->xmz", table, field, precision=highest)
    shape = field.shape
    blocked = table.shape[1]
    grid = field.reshape(shape[0], shape[1], shape[2] // blocked, blocked)
    result = jnp.einsum("mk,xynk->xynm", table, grid, precision=highest)
    return result.reshape(shape[0], shape[1], -1)


def shift(value, dw, dd):
    nw = lax.axis_size("wide")
    nd = lax.axis_size("deep")
    if dd == 0:
        pairs = [((w + dw) % nw, w) for w in range(nw)]
        return lax.ppermute(value, "wide", pairs)
    if dw == 0:
        pairs = [((d + dd) % nd, d) for d in range(nd)]
        return lax.ppermute(value, "deep", pairs)
    pairs = []
    for w in range(nw):
        for d in range(nd):
            src = ((w + dw) % nw) * nd + (d + dd) % nd
            pairs.append((src, w * nd + d))
    return lax.ppermute(value, ("wide", "deep"), pairs)


def node_mask(length, count, node, axis, ndim):
    index = lax.broadcasted_iota(jnp.int32, (length,), 0) % count == node
    shape = [1] * ndim
    shape[axis] = length
    return index.reshape(shape)


def assemble(field, count, carry=None):
    nd = field.ndim
    X, Y, Z = field.shape[-3:]
    lx = shift(field[..., -1, :, :], -1, 0)
    rx = shift(field[..., 0, :, :], 1, 0)
    ext = jnp.concatenate([lx[..., None, :, :], field, rx[..., None, :, :]], axis=-3)
    hi = node_mask(X, count, count - 1, nd - 3, nd)
    lo = node_mask(X, count, 0, nd - 3, nd)
    field = (
        ext[..., 1 : X + 1, :, :]
        + jnp.where(hi, ext[..., 2 : X + 2, :, :], 0.0)
        + jnp.where(lo, ext[..., 0:X, :, :], 0.0)
    )
    ly = shift(field[..., :, -1, :], 0, -1)
    face = field[..., :, 0, :]
    carried = None
    if carry is None:
        ry = shift(face, 0, 1)
    else:
        packed = shift(jnp.concatenate([face.reshape(-1), carry]), 0, 1)
        ry = packed[: face.size].reshape(face.shape)
        carried = packed[face.size :]
    ext = jnp.concatenate([ly[..., :, None, :], field, ry[..., :, None, :]], axis=-2)
    hi = node_mask(Y, count, count - 1, nd - 2, nd)
    lo = node_mask(Y, count, 0, nd - 2, nd)
    field = (
        ext[..., :, 1 : Y + 1, :]
        + jnp.where(hi, ext[..., :, 2 : Y + 2, :], 0.0)
        + jnp.where(lo, ext[..., :, 0:Y, :], 0.0)
    )
    hi = node_mask(Z, count, count - 1, nd - 1, nd)
    lo = node_mask(Z, count, 0, nd - 1, nd)
    field = (
        field
        + jnp.where(hi, jnp.roll(field, -1, axis=-1), 0.0)
        + jnp.where(lo, jnp.roll(field, 1, axis=-1), 0.0)
    )
    if carry is None:
        return field
    return field, carried


def apply_operator(field, metric, helm, tables):
    shape = field.shape
    flat = field.reshape(-1, shape[-1])
    total = helm.reshape(flat.shape) * flat
    tx, ty, tz = tables
    for axis, table in ((0, tx), (1, ty)):
        slope = jnp.dot(table, flat, precision=fast)
        weighted = metric[axis].reshape(flat.shape) * slope
        total = total + jnp.dot(table.T, weighted, precision=fast)
    slope = jnp.dot(flat, tz.T, precision=fast)
    weighted = metric[2].reshape(flat.shape) * slope
    total = total + jnp.dot(weighted, tz, precision=fast)
    return total.reshape(shape)


def big_tables(small, shape):
    X, Y, Z = shape
    n = small.shape[0]
    px = np.kron(np.kron(np.eye(X // n, dtype=np.float32), small), np.eye(Y, dtype=np.float32))
    py = np.kron(np.eye(X, dtype=np.float32), np.kron(np.eye(Y // n, dtype=np.float32), small))
    pz = np.kron(np.eye(Z // n, dtype=np.float32), small)
    return tuple(jnp.asarray(t) for t in (px, py, pz))


def chebyshev(solution, rhs_local, metric, helm, tables, inverse, first_residual):
    centre = (upper_bound + lower_bound) / 2.0
    half_width = (upper_bound - lower_bound) / 2.0
    aspect = centre / half_width
    weight_prev = 1.0 / aspect
    if first_residual is not None:
        residual = first_residual
    else:
        residual = assemble(rhs_local - apply_operator(solution, metric, helm, tables), NP)
    update = inverse * residual / centre
    solution = solution + update
    residual = assemble(rhs_local - apply_operator(solution, metric, helm, tables), NP)
    weight_next = 1.0 / (2.0 * aspect - weight_prev)
    update = (
        weight_next * weight_prev * update + 2.0 * weight_next / half_width * inverse * residual
    )
    solution = solution + update
    return solution


def local(rhs_local, metric, helm, columns, live_blocks, block_values):
    derivative, linear = gll_tables(NP)
    shape = rhs_local.shape
    nw = lax.axis_size("wide")
    copies = (shape[0] // NP, shape[1] // NP, block_extent() // NP)
    tables = big_tables(derivative, shape)
    sx, sy, sz = big_tables(derivative * derivative, shape)
    down_tables = tuple((repeat_table(linear.T, copies[axis]) for axis in range(3)))
    up_tables = tuple((repeat_table(linear, copies[axis]) for axis in range(3)))

    rows = shape[0] * shape[1]
    diagonal = (
        helm.reshape(rows, -1)
        + jnp.dot(sx.T, metric[0].reshape(rows, -1), precision=fast)
        + jnp.dot(sy.T, metric[1].reshape(rows, -1), precision=fast)
        + jnp.dot(metric[2].reshape(rows, -1), sz, precision=fast)
    ).reshape(shape)
    mats = jnp.concatenate(
        [
            block_values[0, 0].reshape(-1),
            columns[0, 0].astype(jnp.float32).reshape(-1),
            live_blocks[0, 0].astype(jnp.float32),
        ]
    )
    both, mats = assemble(jnp.stack([diagonal, rhs_local]), NP, mats)
    nvals = block_values.shape[2] * block_values.shape[3]
    ncols = columns.shape[2] * columns.shape[3]
    next_values = mats[:nvals].reshape(block_values.shape[2:])
    next_columns = mats[nvals : nvals + ncols].astype(jnp.int32).reshape(columns.shape[2:])
    next_live = mats[nvals + ncols :].astype(jnp.int32)
    inverse = 1.0 / both[0]
    first = chebyshev(
        jnp.zeros_like(rhs_local), rhs_local, metric, helm, tables, inverse, both[1]
    )
    local_res = rhs_local - apply_operator(first, metric, helm, tables)
    corners = local_res
    for axis in range(3):
        corners = contract(corners, down_tables[axis], axis)

    cx, cy, cz = corners.shape
    ext = jnp.concatenate([shift(corners, 0, -1), corners, shift(corners, 0, 1)], axis=1)
    qz = ext[:, :, 0::2] + jnp.roll(ext, 1, axis=2)[:, :, 0::2]
    qy = qz[:, cy : cy + 7 : 2] + qz[:, cy - 1 : cy + 6 : 2]
    zero = jnp.zeros_like(qy[:1])
    qx = jnp.concatenate([zero, qy, zero], axis=0)
    partial = qx[1 : cx + 2 : 2] + qx[0 : cx + 1 : 2]

    sent = jnp.stack(
        [jnp.roll(partial, 1, axis=2), partial, jnp.roll(partial, -1, axis=2)], axis=-1
    )
    sent = jnp.transpose(sent, (2, 0, 1, 3))
    got = lax.all_to_all(sent, "wide", 0, 0, tiled=True)
    even = got[:, 0] + jnp.roll(got[:, 2], 1, axis=0)
    got = jnp.stack([even, got[:, 1]], axis=1)
    frame = jnp.transpose(got, (3, 2, 0, 1)).reshape(3, 4, -1)
    span = frame.shape[2]
    nxb = span // BS
    frame_rows = frame.reshape(-1, BS)

    cols = jnp.concatenate([columns[0], next_columns[None]], axis=0)
    lives = jnp.concatenate([live_blocks[0], next_live[None]], axis=0)
    vals = jnp.concatenate([block_values[0], next_values[None]], axis=0)
    y_off = jnp.array([0, 0, 2], jnp.int32)[:, None, None]
    layer = cols // (2 * nxb)
    block = cols % (2 * nxb)
    index = (layer * 4 + y_off + block // nxb) * nxb + block % nxb
    picked = jnp.take(frame_rows, index.reshape(-1), axis=0).reshape(index.shape + (BS,))
    live = (jnp.arange(K, dtype=jnp.int32)[None, None, :] < lives[:, :, None]).astype(
        jnp.float32
    )
    values = vals.reshape(vals.shape[:2] + (K, BS, BS))
    product = jnp.einsum("yxkij,yxkj,yxk->yxi", values, picked, live, precision=highest)
    product = product.reshape(3, span)
    coarse_product = product[:2].reshape(1, 2, span)

    back = jnp.stack(
        [product[:, 0::2], product[:, 1::2], jnp.roll(product, -2, axis=1)[:, 0::2]], axis=-1
    )
    back = jnp.transpose(back, (1, 0, 2))
    got = lax.all_to_all(back, "wide", 0, 0, tiled=True)
    hx = jnp.stack([got[:, :, 0:2], got[:, :, 1:3]], axis=-1).reshape(nw, 3, 4)
    hy = jnp.stack([hx[:, 0:2], hx[:, 1:3]], axis=2).reshape(nw, 4, 4)
    hz = jnp.stack([hy, jnp.roll(hy, -1, axis=0)], axis=1).reshape(2 * nw, 4, 4)
    correction = jnp.transpose(hz, (2, 1, 0))
    for axis in range(3):
        correction = contract(correction, up_tables[axis], axis)
    second = first + correction
    smoothed = chebyshev(second, rhs_local, metric, helm, tables, inverse, None)
    return (smoothed, coarse_product)


def solution(mesh):
    placed = (
        P("wide", "deep", None),
        P(None, "wide", "deep", None),
        P("wide", "deep", None),
        P("wide", "deep", None, None),
        P("wide", "deep", None),
        P("wide", "deep", None, None),
    )
    return jax.shard_map(
        local,
        mesh=mesh,
        in_specs=placed,
        out_specs=(P("wide", "deep", None), P("wide", "deep", None)),
        check_vma=False,
    )
```

```python
import jax
import jax.numpy as jnp
import numpy as np
from jax import lax
from jax.sharding import PartitionSpec as P

NP = 8
K = 8
BS = 8


upper_bound = 6.0
lower_bound = 0.6
highest = lax.Precision.HIGHEST
fast = lax.Precision.HIGH


def gll_tables(count):
    order = count - 1
    nodes = np.cos(np.pi * np.arange(count) / order)
    legendre = np.zeros((count, count))
    for sweep in range(101):
        legendre[:, 0] = 1.0
        legendre[:, 1] = nodes
        for degree in range(2, count):
            legendre[:, degree] = (
                (2 * degree - 1) * nodes * legendre[:, degree - 1]
                - (degree - 1) * legendre[:, degree - 2]
            ) / degree
        if sweep < 100:
            nodes = nodes - (nodes * legendre[:, order] - legendre[:, order - 1]) / (
                count * legendre[:, order]
            )
    nodes = nodes[::-1].copy()
    values = legendre[::-1, order].copy()
    identity_table = np.eye(count)
    spacing = nodes[:, None] - nodes[None, :] + identity_table
    derivative = values[:, None] / values[None, :] / spacing
    derivative = derivative * (1.0 - identity_table)
    derivative[0, 0] = -order * (order + 1) / 4.0
    derivative[-1, -1] = order * (order + 1) / 4.0
    linear = np.stack([(1.0 - nodes) / 2.0, (1.0 + nodes) / 2.0], axis=1)
    return (np.asarray(derivative, np.float32), np.asarray(linear, np.float32))


def block_extent():
    return 128


def repeat_table(small, copies):
    return jnp.asarray(np.kron(np.eye(copies, dtype=np.float32), small))


def contract(field, table, axis):
    if axis == 0:
        return jnp.einsum("mi,iyz->myz", table, field, precision=highest)
    if axis == 1:
        return jnp.einsum("mj,xjz->xmz", table, field, precision=highest)
    shape = field.shape
    blocked = table.shape[1]
    grid = field.reshape(shape[0], shape[1], shape[2] // blocked, blocked)
    result = jnp.einsum("mk,xynk->xynm", table, grid, precision=highest)
    return result.reshape(shape[0], shape[1], -1)


def shift(value, dw, dd):
    nw = lax.axis_size("wide")
    nd = lax.axis_size("deep")
    if dd == 0:
        pairs = [((w + dw) % nw, w) for w in range(nw)]
        return lax.ppermute(value, "wide", pairs)
    if dw == 0:
        pairs = [((d + dd) % nd, d) for d in range(nd)]
        return lax.ppermute(value, "deep", pairs)
    pairs = []
    for w in range(nw):
        for d in range(nd):
            src = ((w + dw) % nw) * nd + (d + dd) % nd
            pairs.append((src, w * nd + d))
    return lax.ppermute(value, ("wide", "deep"), pairs)


def node_mask(length, count, node, axis, ndim):
    index = lax.broadcasted_iota(jnp.int32, (length,), 0) % count == node
    shape = [1] * ndim
    shape[axis] = length
    return index.reshape(shape)


def assemble(field, count, carry=None):
    nd = field.ndim
    X, Y, Z = field.shape[-3:]
    lx = shift(field[..., -1, :, :], -1, 0)
    rx = shift(field[..., 0, :, :], 1, 0)
    ext = jnp.concatenate([lx[..., None, :, :], field, rx[..., None, :, :]], axis=-3)
    hi = node_mask(X, count, count - 1, nd - 3, nd)
    lo = node_mask(X, count, 0, nd - 3, nd)
    field = (
        ext[..., 1 : X + 1, :, :]
        + jnp.where(hi, ext[..., 2 : X + 2, :, :], 0.0)
        + jnp.where(lo, ext[..., 0:X, :, :], 0.0)
    )
    ly = shift(field[..., :, -1, :], 0, -1)
    face = field[..., :, 0, :]
    carried = None
    if carry is None:
        ry = shift(face, 0, 1)
    else:
        packed = shift(jnp.concatenate([face.reshape(-1), carry]), 0, 1)
        ry = packed[: face.size].reshape(face.shape)
        carried = packed[face.size :]
    ext = jnp.concatenate([ly[..., :, None, :], field, ry[..., :, None, :]], axis=-2)
    hi = node_mask(Y, count, count - 1, nd - 2, nd)
    lo = node_mask(Y, count, 0, nd - 2, nd)
    field = (
        ext[..., :, 1 : Y + 1, :]
        + jnp.where(hi, ext[..., :, 2 : Y + 2, :], 0.0)
        + jnp.where(lo, ext[..., :, 0:Y, :], 0.0)
    )
    hi = node_mask(Z, count, count - 1, nd - 1, nd)
    lo = node_mask(Z, count, 0, nd - 1, nd)
    field = (
        field
        + jnp.where(hi, jnp.roll(field, -1, axis=-1), 0.0)
        + jnp.where(lo, jnp.roll(field, 1, axis=-1), 0.0)
    )
    if carry is None:
        return field
    return field, carried


def apply_operator(field, metric, helm, tables):
    shape = field.shape
    flat = field.reshape(-1, shape[-1])
    total = helm.reshape(flat.shape) * flat
    tx, ty, tz = tables
    for axis, table in ((0, tx), (1, ty)):
        slope = jnp.dot(table, flat, precision=fast)
        weighted = metric[axis].reshape(flat.shape) * slope
        total = total + jnp.dot(table.T, weighted, precision=fast)
    slope = jnp.dot(flat, tz.T, precision=fast)
    weighted = metric[2].reshape(flat.shape) * slope
    total = total + jnp.dot(weighted, tz, precision=fast)
    return total.reshape(shape)


def big_tables(small, shape):
    X, Y, Z = shape
    n = small.shape[0]
    px = np.kron(np.kron(np.eye(X // n, dtype=np.float32), small), np.eye(Y, dtype=np.float32))
    py = np.kron(np.eye(X, dtype=np.float32), np.kron(np.eye(Y // n, dtype=np.float32), small))
    pz = np.kron(np.eye(Z // n, dtype=np.float32), small)
    return tuple(jnp.asarray(t) for t in (px, py, pz))


def chebyshev(solution, rhs_local, metric, helm, tables, inverse, first_residual):
    centre = (upper_bound + lower_bound) / 2.0
    half_width = (upper_bound - lower_bound) / 2.0
    aspect = centre / half_width
    weight_prev = 1.0 / aspect
    if first_residual is not None:
        residual = first_residual
    else:
        residual = assemble(rhs_local - apply_operator(solution, metric, helm, tables), NP)
    update = inverse * residual / centre
    solution = solution + update
    residual = assemble(rhs_local - apply_operator(solution, metric, helm, tables), NP)
    weight_next = 1.0 / (2.0 * aspect - weight_prev)
    update = (
        weight_next * weight_prev * update + 2.0 * weight_next / half_width * inverse * residual
    )
    solution = solution + update
    return solution


def local(rhs_local, metric, helm, columns, live_blocks, block_values):
    derivative, linear = gll_tables(NP)
    shape = rhs_local.shape
    nw = lax.axis_size("wide")
    copies = (shape[0] // NP, shape[1] // NP, block_extent() // NP)
    tables = big_tables(derivative, shape)
    sx, sy, sz = big_tables(derivative * derivative, shape)
    down_tables = tuple((repeat_table(linear.T, copies[axis]) for axis in range(3)))
    up_tables = tuple((repeat_table(linear, copies[axis]) for axis in range(3)))

    rows = shape[0] * shape[1]
    diagonal = (
        helm.reshape(rows, -1)
        + jnp.dot(sx.T, metric[0].reshape(rows, -1), precision=fast)
        + jnp.dot(sy.T, metric[1].reshape(rows, -1), precision=fast)
        + jnp.dot(metric[2].reshape(rows, -1), sz, precision=fast)
    ).reshape(shape)
    mats = jnp.concatenate(
        [
            block_values[0, 0].reshape(-1),
            columns[0, 0].astype(jnp.float32).reshape(-1),
            live_blocks[0, 0].astype(jnp.float32),
        ]
    )
    both, mats = assemble(jnp.stack([diagonal, rhs_local]), NP, mats)
    nvals = block_values.shape[2] * block_values.shape[3]
    ncols = columns.shape[2] * columns.shape[3]
    next_values = mats[:nvals].reshape(block_values.shape[2:])
    next_columns = mats[nvals : nvals + ncols].astype(jnp.int32).reshape(columns.shape[2:])
    next_live = mats[nvals + ncols :].astype(jnp.int32)
    inverse = 1.0 / both[0]
    first = chebyshev(
        jnp.zeros_like(rhs_local), rhs_local, metric, helm, tables, inverse, both[1]
    )
    local_res = rhs_local - apply_operator(first, metric, helm, tables)
    corners = local_res
    for axis in range(3):
        corners = contract(corners, down_tables[axis], axis)

    cx, cy, cz = corners.shape
    ext = jnp.concatenate([shift(corners, 0, -1), corners, shift(corners, 0, 1)], axis=1)
    qz = ext[:, :, 0::2] + jnp.roll(ext, 1, axis=2)[:, :, 0::2]
    qy = qz[:, cy : cy + 7 : 2] + qz[:, cy - 1 : cy + 6 : 2]
    zero = jnp.zeros_like(qy[:1])
    qx = jnp.concatenate([zero, qy, zero], axis=0)
    partial = qx[1 : cx + 2 : 2] + qx[0 : cx + 1 : 2]

    sent = jnp.stack(
        [jnp.roll(partial, 1, axis=2), partial, jnp.roll(partial, -1, axis=2)], axis=-1
    )
    sent = jnp.transpose(sent, (2, 0, 1, 3))
    got = lax.all_to_all(sent, "wide", 0, 0, tiled=True)
    even = got[:, 0] + jnp.roll(got[:, 2], 1, axis=0)
    got = jnp.stack([even, got[:, 1]], axis=1)
    frame = jnp.transpose(got, (3, 2, 0, 1)).reshape(3, 4, -1)
    span = frame.shape[2]
    nxb = span // BS
    frame_rows = frame.reshape(-1, BS)

    cols = jnp.concatenate([columns[0], next_columns[None]], axis=0)
    lives = jnp.concatenate([live_blocks[0], next_live[None]], axis=0)
    vals = jnp.concatenate([block_values[0], next_values[None]], axis=0)
    y_off = jnp.array([0, 0, 2], jnp.int32)[:, None, None]
    layer = cols // (2 * nxb)
    block = cols % (2 * nxb)
    index = (layer * 4 + y_off + block // nxb) * nxb + block % nxb
    picked = jnp.take(frame_rows, index.reshape(-1), axis=0, mode="clip").reshape(index.shape + (BS,))
    live = (jnp.arange(K, dtype=jnp.int32)[None, None, :] < lives[:, :, None]).astype(
        jnp.float32
    )
    values = vals.reshape(vals.shape[:2] + (K, BS, BS))
    product = jnp.einsum("yxkij,yxkj,yxk->yxi", values, picked, live, precision=highest)
    product = product.reshape(3, span)
    coarse_product = product[:2].reshape(1, 2, span)

    back = jnp.stack(
        [product[:, 0::2], product[:, 1::2], jnp.roll(product, -2, axis=1)[:, 0::2]], axis=-1
    )
    back = jnp.transpose(back, (1, 0, 2))
    got = lax.all_to_all(back, "wide", 0, 0, tiled=True)
    hx = jnp.stack([got[:, :, 0:2], got[:, :, 1:3]], axis=-1).reshape(nw, 3, 4)
    hy = jnp.stack([hx[:, 0:2], hx[:, 1:3]], axis=2).reshape(nw, 4, 4)
    hz = jnp.stack([hy, jnp.roll(hy, -1, axis=0)], axis=1).reshape(2 * nw, 4, 4)
    correction = jnp.transpose(hz, (2, 1, 0))
    for axis in range(3):
        correction = contract(correction, up_tables[axis], axis)
    second = first + correction
    smoothed = chebyshev(second, rhs_local, metric, helm, tables, inverse, None)
    return (smoothed, coarse_product)


def solution(mesh):
    placed = (
        P("wide", "deep", None),
        P(None, "wide", "deep", None),
        P("wide", "deep", None),
        P("wide", "deep", None, None),
        P("wide", "deep", None),
        P("wide", "deep", None, None),
    )
    return jax.shard_map(
        local,
        mesh=mesh,
        in_specs=placed,
        out_specs=(P("wide", "deep", None), P("wide", "deep", None)),
        check_vma=False,
    )
```
